512 devices in a mesh: wide: 32 (over z, x), narrow: 16 (over y, core).
Axes of the slice: x: 4, y: 8, z: 8, core: 2. Of those that a mesh axis runs over, the one named last changes fastest.
Arguments:
- a_blocks: bfloat16 [8192, 3, 128, 128], P(('wide', 'narrow')), may hold values from -6 to 6
- a_cols: int32 [8192, 3], P(('wide', 'narrow')), may hold values from 0 to 255, as said below
- prolong: bfloat16 [8192, 128, 128], P(('wide', 'narrow')), may hold values from -0.5 to 0.5
- owners: int32 [8192], P(('wide', 'narrow')), may hold values from 0 to 31, as said below
- slots: int32 [8192, 3], P(('wide', 'narrow')), may hold values from 0 to 23
Outputs:
- coarse: float32 [12288, 128, 128], P(('wide', 'narrow'))
The draws below stay inside these ranges and needn't reach their ends.
Inputs may be any that keep to these rules, and one draw needn't show every extreme that they name: `a_cols`: the first entry of every block row is the block row itself (n * 16 + r). The other entries of one device's block rows name fine block rows of any one device of its narrow group at most 8 times, and in every narrow group one device is named exactly 8 times by every device of the group. `owners`: the block rows of one device name one owner at most 2 times; for every narrow index, one owner is named exactly 2 times by every device with that narrow index.
All inputs are finite; a program needn't handle non-finite values.
Results may differ from the reference program's by a relative error of at most 0.0041.
Values may be sent and summed in bfloat16 or wider, within the bound.
No kernel may reach another device: no remote copies, remote signals or barrier semaphores. Data moves between devices by JAX's collectives and lax.ppermute only.
A program may use at most 64 MiB of HBM per device.

```python
import jax
import jax.numpy as jnp
from jax import lax

B = 128
K = 3
RB = 16
CAP_OWNER = 2
CAP_PEER = 8
CB_DEV = 24
GROUP = 256
FINE = 8192
COARSE = 12288
N_WIDE = 32
N_NARROW = 16


def draw_a_cols(key, part):
    devices = N_WIDE * N_NARROW
    busiest = jax.random.randint(jax.random.fold_in(key, 11), (N_WIDE,), 0, N_NARROW).astype(jnp.int32)
    device_keys = jax.random.split(jax.random.fold_in(key, 12), devices)

    def slab_cols(device, device_key):
        hot_peer = busiest[device // N_NARROW]
        key_perm, key_order, key_local = jax.random.split(device_key, 3)
        off_count = (K - 1) * RB
        shuffled = jax.random.permutation(key_perm, (N_NARROW - 1) * CAP_PEER)[:off_count - CAP_PEER]
        other_peers = (shuffled // CAP_PEER).astype(jnp.int32)
        other_peers = other_peers + (other_peers >= hot_peer).astype(jnp.int32)
        peer_list = jnp.concatenate([jnp.full((CAP_PEER,), hot_peer, jnp.int32), other_peers])
        peer_list = peer_list[jax.random.permutation(key_order, off_count)]
        local_index = jax.random.randint(key_local, (off_count,), 0, RB).astype(jnp.int32)
        off_cols = (peer_list * RB + local_index).reshape(RB, K - 1)
        diagonal_cols = (device % N_NARROW * RB + jnp.arange(RB, dtype=jnp.int32))[:, None]
        return jnp.concatenate([diagonal_cols, off_cols], axis=1).astype(jnp.int32)
    columns = jax.vmap(slab_cols)(jnp.arange(devices, dtype=jnp.int32), device_keys)
    return columns.reshape(devices * RB, K)


def draw_owners(key, part):
    devices = N_WIDE * N_NARROW
    busiest = jax.random.randint(jax.random.fold_in(key, 21), (N_NARROW,), 0, N_WIDE).astype(jnp.int32)
    device_keys = jax.random.split(jax.random.fold_in(key, 22), devices)

    def slab_owners(device, device_key):
        hot_owner = busiest[device % N_NARROW]
        key_perm, key_order = jax.random.split(device_key, 2)
        shuffled = jax.random.permutation(key_perm, (N_WIDE - 1) * CAP_OWNER)[:RB - CAP_OWNER]
        other_owners = (shuffled // CAP_OWNER).astype(jnp.int32)
        other_owners = other_owners + (other_owners >= hot_owner).astype(jnp.int32)
        owner_list = jnp.concatenate([jnp.full((CAP_OWNER,), hot_owner, jnp.int32), other_owners])
        return owner_list[jax.random.permutation(key_order, RB)].astype(jnp.int32)
    listing = jax.vmap(slab_owners)(jnp.arange(devices, dtype=jnp.int32), device_keys)
    return listing.reshape(devices * RB)


def touch_ends(values, stream_key, least, top_value):
    longest = values.shape.index(max(values.shape))
    spots = []
    for shift in (0, 1):
        where = [jax.random.randint(jax.random.fold_in(stream_key, axis), (), 0, length) for axis, length in enumerate(values.shape)]
        where[longest] = (where[longest] + shift) % values.shape[longest]
        spots.append(tuple(where))
    return values.at[spots[0]].set(least).at[spots[1]].set(top_value)


def block_levels(key, dims, cuts, low, largest):
    loudness = 1.0
    for position, shards_of in cuts:
        heights = jax.random.uniform(jax.random.fold_in(jax.random.fold_in(key, 6), position), (shards_of,), jnp.float32, low / len(cuts), largest / len(cuts))
        loudness = loudness * jnp.repeat(jnp.exp(heights), dims[position] // shards_of).reshape((-1,) + (1,) * (len(dims) - 1 - position))
    return loudness


def noise(key, extent, deviation, limit, shards=(), held_as=jnp.bfloat16):
    loudness = block_levels(key, extent, shards, -0.22, 0.18) if shards else 1.0
    array = jax.random.normal(key, extent, jnp.float32) * deviation * loudness
    return jnp.minimum(jnp.maximum(array, -limit), limit).astype(held_as)


def setup_inputs(seed: int = 0) -> dict:
    arg_keys = jax.random.split(jax.random.key(seed), 6)
    a_blocks = noise(arg_keys[0], (FINE, K, B, B), 1.0, 6.0, ((0, 512),))
    a_cols = draw_a_cols(jax.random.fold_in(arg_keys[5], 71), 0)
    prolong = noise(arg_keys[2], (FINE, B, B), B ** -0.5, 0.5, ((0, 512),))
    owners = draw_owners(jax.random.fold_in(arg_keys[5], 71), 0)
    slots = touch_ends(jax.random.randint(arg_keys[4], (FINE, K), 0, CB_DEV), jax.random.fold_in(arg_keys[4], 1), 0, CB_DEV - 1).astype(jnp.int32)
    return dict(a_blocks=a_blocks, a_cols=a_cols, prolong=prolong, owners=owners, slots=slots)


def reference(a_blocks, a_cols, prolong, owners, slots):
    devices = N_WIDE * N_NARROW
    a_slabs = a_blocks.reshape(devices, RB, K, B, B)
    col_slabs = a_cols.reshape(devices, RB, K)
    prolong_slabs = prolong.reshape(devices, RB, B, B)
    owner_slabs = owners.reshape(devices, RB)
    slot_slabs = slots.reshape(devices, RB, K)

    def add_slab(coarse_sum, inputs):
        device, a_slab, col_slab, prolong_slab, owner_slab, slot_slab = inputs
        wide_index = device // N_NARROW
        narrow_index = device % N_NARROW
        global_cols = (wide_index * GROUP + col_slab).astype(jnp.int32).reshape(-1)
        right_blocks = jnp.take(prolong, global_cols, axis=0).reshape(RB, K, B, B)
        product = jnp.einsum("rkij,rkjl->rkil", a_slab.astype(jnp.float32), right_blocks.astype(jnp.float32)).astype(jnp.bfloat16)
        product = lax.optimization_barrier(product)
        galerkin = jnp.einsum("rji,rkjl->rkil", prolong_slab.astype(jnp.float32), product.astype(jnp.float32)).astype(jnp.bfloat16)
        galerkin = lax.optimization_barrier(galerkin)
        target_index = ((owner_slab[:, None] * N_NARROW + narrow_index) * CB_DEV + slot_slab).astype(jnp.int32).reshape(-1)
        coarse_sum = coarse_sum.at[target_index].add(galerkin.reshape(RB * K, B, B).astype(jnp.float32))
        return coarse_sum, None

    start_sum = jnp.zeros((COARSE, B, B), jnp.float32)
    device_ids = jnp.arange(devices, dtype=jnp.int32)
    coarse_sum, unused = lax.scan(add_slab, start_sum, (device_ids, a_slabs, col_slabs, prolong_slabs, owner_slabs, slot_slabs))
    return coarse_sum
```

```python
import jax
import jax.numpy as jnp
from jax import lax
from jax.sharding import PartitionSpec as P

CAP_OWNER = 2
CB_DEV = 24


def galerkin_of(left, right, prolong_rows):
    product = jnp.einsum(
        "rkij,rkjl->rkil", left, right, preferred_element_type=jnp.float32
    ).astype(jnp.bfloat16)
    return jnp.einsum(
        "rji,rkjl->rkil", prolong_rows, product, preferred_element_type=jnp.float32
    ).astype(jnp.bfloat16)


def bucket_blocks(bucket_map, galerkin, owner_count):
    slab_rows, per_row, block_size, unused_size = galerkin.shape
    outgoing = jnp.dot(
        bucket_map.astype(jnp.bfloat16),
        galerkin.reshape(slab_rows, per_row * block_size * block_size),
        preferred_element_type=jnp.float32,
    )
    return outgoing.astype(jnp.bfloat16).reshape(
        owner_count, CAP_OWNER * per_row, block_size, block_size
    )


def per_device(a_blocks, a_cols, prolong, owners, slots):
    slab_rows, per_row, block_size, unused_size = a_blocks.shape
    owner_count = lax.axis_size("wide")

    row_ids = jnp.arange(slab_rows, dtype=jnp.int32)
    same_owner = (owners[:, None] == owners[None, :]) & (row_ids[None, :] < row_ids[:, None])
    owner_position = jnp.sum(same_owner.astype(jnp.int32), axis=1)
    bucket = owners * CAP_OWNER + owner_position
    bucket_map = jnp.arange(owner_count * CAP_OWNER, dtype=jnp.int32)[:, None] == bucket[None, :]
    outgoing_slots = (
        jnp.sum(jnp.where(bucket_map[:, :, None], slots[None, :, :] + 1, 0), axis=1) - 1
    )
    outgoing_slots = outgoing_slots.reshape(owner_count, CAP_OWNER, per_row)
    arrived_slots = lax.all_to_all(outgoing_slots, "wide", split_axis=0, concat_axis=0, tiled=True)

    galerkin_diag = galerkin_of(a_blocks[:, :1], prolong[:, None], prolong)
    outgoing_diag = bucket_blocks(bucket_map, galerkin_diag, owner_count)
    arrived_diag = lax.all_to_all(outgoing_diag, "wide", split_axis=0, concat_axis=0, tiled=True)

    shard_blocks = lax.all_gather(prolong, "narrow", axis=0, tiled=True)
    piece_rows = shard_blocks.shape[0]
    off_cols = jnp.clip(a_cols[:, 1:].reshape(-1), 0, piece_rows - 1)
    right_blocks = jnp.take(shard_blocks, off_cols, axis=0).reshape(
        slab_rows, per_row - 1, block_size, block_size
    )
    galerkin_off = galerkin_of(a_blocks[:, 1:], right_blocks, prolong)
    outgoing_off = bucket_blocks(bucket_map, galerkin_off, owner_count)
    arrived_off = lax.all_to_all(outgoing_off, "wide", split_axis=0, concat_axis=0, tiled=True)

    slots_diag = arrived_slots[:, :, :1].reshape(-1)
    slots_off = arrived_slots[:, :, 1:].reshape(-1)
    slot_ids = jnp.arange(CB_DEV, dtype=jnp.int32)[:, None]
    coarse_sum = jnp.dot(
        (slot_ids == slots_diag[None, :]).astype(jnp.bfloat16),
        arrived_diag.reshape(-1, block_size * block_size),
        preferred_element_type=jnp.float32,
    ) + jnp.dot(
        (slot_ids == slots_off[None, :]).astype(jnp.bfloat16),
        arrived_off.reshape(-1, block_size * block_size),
        preferred_element_type=jnp.float32,
    )
    return coarse_sum.reshape(CB_DEV, block_size, block_size)


def solution(mesh):
    return jax.shard_map(
        per_device,
        mesh=mesh,
        in_specs=(
            P(("wide", "narrow"), None, None, None),
            P(("wide", "narrow"), None),
            P(("wide", "narrow"), None, None),
            P(("wide", "narrow")),
            P(("wide", "narrow"), None),
        ),
        out_specs=P(("wide", "narrow"), None, None),
        check_vma=False,
    )
```

```python
import functools

import jax
import jax.numpy as jnp
from jax import lax
from jax.experimental import pallas as pl
from jax.experimental.pallas import tpu as pltpu
from jax.sharding import PartitionSpec as P

CAP_OWNER = 2
CB_DEV = 24


def galerkin_kernel(n_k, bucket_ref, cols_ref, *refs):
    a_refs = refs[:n_k]
    right_refs = refs[n_k:2 * n_k]
    pt_ref = refs[2 * n_k]
    out_ref = refs[2 * n_k + 1]
    row = pl.program_id(0)

    @pl.when(row == 0)
    def _():
        out_ref[...] = jnp.zeros_like(out_ref)

    bucket = bucket_ref[row]
    for k in range(n_k):
        product = jnp.dot(
            a_refs[k][...], right_refs[k][...], preferred_element_type=jnp.float32
        ).astype(jnp.bfloat16)
        galerkin = jnp.dot(pt_ref[...], product, preferred_element_type=jnp.float32)
        out_ref[bucket, k] = galerkin.astype(jnp.bfloat16)


def galerkin_buckets(a_blocks, ks, table, cols, prolong_t, bucket, bucket_count):
    slab_rows, unused_k, block_size, unused_size = a_blocks.shape
    n_k = len(ks)
    squeezed = pl.Squeezed()
    a_specs = [
        pl.BlockSpec((squeezed, squeezed, block_size, block_size),
                     functools.partial(lambda k, r, b, c: (r, k, 0, 0), k))
        for k in ks
    ]
    right_specs = [
        pl.BlockSpec((squeezed, block_size, block_size),
                     functools.partial(lambda j, r, b, c: (c[r, j], 0, 0), j))
        for j in range(n_k)
    ]
    pt_spec = pl.BlockSpec((squeezed, block_size, block_size), lambda r, b, c: (r, 0, 0))
    out_spec = pl.BlockSpec(
        (bucket_count, n_k, block_size, block_size), lambda r, b, c: (0, 0, 0, 0)
    )
    flops = 4 * slab_rows * n_k * block_size ** 3
    moved = 2 * block_size * block_size * (slab_rows * (2 * n_k + 1) + bucket_count * n_k)
    return pl.pallas_call(
        functools.partial(galerkin_kernel, n_k),
        out_shape=jax.ShapeDtypeStruct((bucket_count, n_k, block_size, block_size), jnp.bfloat16),
        grid_spec=pltpu.PrefetchScalarGridSpec(
            num_scalar_prefetch=2,
            grid=(slab_rows,),
            in_specs=a_specs * 1 + right_specs + [pt_spec],
            out_specs=out_spec,
        ),
        compiler_params=pltpu.CompilerParams(dimension_semantics=("arbitrary",)),
        cost_estimate=pl.CostEstimate(flops=flops, bytes_accessed=moved, transcendentals=0),
    )(bucket, cols, *([a_blocks] * n_k), *([table] * n_k), prolong_t)


def per_device(a_blocks, a_cols, prolong, owners, slots):
    slab_rows, per_row, block_size, unused_size = a_blocks.shape
    owner_count = lax.axis_size("wide")
    bucket_count = owner_count * CAP_OWNER

    row_ids = jnp.arange(slab_rows, dtype=jnp.int32)
    same_owner = (owners[:, None] == owners[None, :]) & (row_ids[None, :] < row_ids[:, None])
    owner_position = jnp.sum(same_owner.astype(jnp.int32), axis=1)
    bucket = jnp.clip(owners * CAP_OWNER + owner_position, 0, bucket_count - 1).astype(jnp.int32)
    bucket_map = jnp.arange(bucket_count, dtype=jnp.int32)[:, None] == bucket[None, :]
    outgoing_slots = (
        jnp.sum(jnp.where(bucket_map[:, :, None], slots[None, :, :] + 1, 0), axis=1) - 1
    )
    outgoing_slots = outgoing_slots.reshape(owner_count, CAP_OWNER, per_row)
    arrived_slots = lax.all_to_all(outgoing_slots, "wide", split_axis=0, concat_axis=0, tiled=True)

    prolong_t = jnp.swapaxes(prolong, 1, 2)

    outgoing_diag = galerkin_buckets(
        a_blocks, (0,), prolong, row_ids[:, None], prolong_t, bucket, bucket_count
    ).reshape(owner_count, CAP_OWNER, block_size, block_size)
    arrived_diag = lax.all_to_all(outgoing_diag, "wide", split_axis=0, concat_axis=0, tiled=True)

    shard_blocks = lax.all_gather(prolong, "narrow", axis=0, tiled=True)
    piece_rows = shard_blocks.shape[0]
    off_cols = jnp.clip(a_cols[:, 1:], 0, piece_rows - 1).astype(jnp.int32)
    outgoing_off = galerkin_buckets(
        a_blocks, tuple(range(1, per_row)), shard_blocks, off_cols, prolong_t, bucket, bucket_count
    ).reshape(owner_count, CAP_OWNER * (per_row - 1), block_size, block_size)
    arrived_off = lax.all_to_all(outgoing_off, "wide", split_axis=0, concat_axis=0, tiled=True)

    slots_diag = arrived_slots[:, :, :1].reshape(-1)
    slots_off = arrived_slots[:, :, 1:].reshape(-1)
    slot_ids = jnp.arange(CB_DEV, dtype=jnp.int32)[:, None]
    coarse_sum = jnp.dot(
        (slot_ids == slots_diag[None, :]).astype(jnp.bfloat16),
        arrived_diag.reshape(-1, block_size * block_size),
        preferred_element_type=jnp.float32,
    ) + jnp.dot(
        (slot_ids == slots_off[None, :]).astype(jnp.bfloat16),
        arrived_off.reshape(-1, block_size * block_size),
        preferred_element_type=jnp.float32,
    )
    return coarse_sum.reshape(CB_DEV, block_size, block_size)


def solution(mesh):
    return jax.shard_map(
        per_device,
        mesh=mesh,
        in_specs=(
            P(("wide", "narrow"), None, None, None),
            P(("wide", "narrow"), None),
            P(("wide", "narrow"), None, None),
            P(("wide", "narrow")),
            P(("wide", "narrow"), None),
        ),
        out_specs=P(("wide", "narrow"), None, None),
        check_vma=False,
    )
```

```python
import functools

import jax
import jax.numpy as jnp
from jax import lax
from jax.experimental import pallas as pl
from jax.experimental.pallas import tpu as pltpu
from jax.sharding import PartitionSpec as P

CAP_OWNER = 2
CB_DEV = 24


ROWS_PER_STEP = 4


def galerkin_kernel(n_k, bucket_ref, cols_ref, *refs):
    a_refs = refs[:n_k]
    right_refs = refs[n_k:n_k + ROWS_PER_STEP * n_k]
    pt_ref = refs[n_k + ROWS_PER_STEP * n_k]
    out_ref = refs[n_k + ROWS_PER_STEP * n_k + 1]
    step = pl.program_id(0)

    @pl.when(step == 0)
    def _():
        out_ref[...] = jnp.zeros_like(out_ref)

    for i in range(ROWS_PER_STEP):
        bucket = bucket_ref[step * ROWS_PER_STEP + i]
        for k in range(n_k):
            product = jnp.dot(
                a_refs[k][i], right_refs[i * n_k + k][...], preferred_element_type=jnp.float32
            ).astype(jnp.bfloat16)
            galerkin = jnp.dot(pt_ref[i], product, preferred_element_type=jnp.float32)
            out_ref[bucket, k] = galerkin.astype(jnp.bfloat16)


def galerkin_buckets(a_blocks, ks, table, cols, prolong_t, bucket, bucket_count):
    slab_rows, unused_k, block_size, unused_size = a_blocks.shape
    n_k = len(ks)
    squeezed = pl.Squeezed()
    a_specs = [
        pl.BlockSpec((ROWS_PER_STEP, squeezed, block_size, block_size),
                     functools.partial(lambda k, s, b, c: (s, k, 0, 0), k))
        for k in ks
    ]
    right_specs = [
        pl.BlockSpec((squeezed, block_size, block_size),
                     functools.partial(lambda i, j, s, b, c: (c[s * ROWS_PER_STEP + i, j], 0, 0), i, j))
        for i in range(ROWS_PER_STEP)
        for j in range(n_k)
    ]
    pt_spec = pl.BlockSpec((ROWS_PER_STEP, block_size, block_size), lambda s, b, c: (s, 0, 0))
    out_spec = pl.BlockSpec(
        (bucket_count, n_k, block_size, block_size), lambda s, b, c: (0, 0, 0, 0)
    )
    flops = 4 * slab_rows * n_k * block_size ** 3
    moved = 2 * block_size * block_size * (slab_rows * (2 * n_k + 1) + bucket_count * n_k)
    return pl.pallas_call(
        functools.partial(galerkin_kernel, n_k),
        out_shape=jax.ShapeDtypeStruct((bucket_count, n_k, block_size, block_size), jnp.bfloat16),
        grid_spec=pltpu.PrefetchScalarGridSpec(
            num_scalar_prefetch=2,
            grid=(slab_rows // ROWS_PER_STEP,),
            in_specs=a_specs + right_specs + [pt_spec],
            out_specs=out_spec,
        ),
        compiler_params=pltpu.CompilerParams(dimension_semantics=("arbitrary",)),
        cost_estimate=pl.CostEstimate(flops=flops, bytes_accessed=moved, transcendentals=0),
    )(bucket, cols, *([a_blocks] * n_k), *([table] * (ROWS_PER_STEP * n_k)), prolong_t)


def per_device(a_blocks, a_cols, prolong, owners, slots):
    slab_rows, per_row, block_size, unused_size = a_blocks.shape
    owner_count = lax.axis_size("wide")
    bucket_count = owner_count * CAP_OWNER

    row_ids = jnp.arange(slab_rows, dtype=jnp.int32)
    same_owner = (owners[:, None] == owners[None, :]) & (row_ids[None, :] < row_ids[:, None])
    owner_position = jnp.sum(same_owner.astype(jnp.int32), axis=1)
    bucket = jnp.clip(owners * CAP_OWNER + owner_position, 0, bucket_count - 1).astype(jnp.int32)
    bucket_map = jnp.arange(bucket_count, dtype=jnp.int32)[:, None] == bucket[None, :]
    outgoing_slots = (
        jnp.sum(jnp.where(bucket_map[:, :, None], slots[None, :, :] + 1, 0), axis=1) - 1
    )
    outgoing_slots = outgoing_slots.reshape(owner_count, CAP_OWNER, per_row)
    arrived_slots = lax.all_to_all(outgoing_slots, "wide", split_axis=0, concat_axis=0, tiled=True)

    prolong_t = jnp.swapaxes(prolong, 1, 2)

    outgoing_diag = galerkin_buckets(
        a_blocks, (0,), prolong, row_ids[:, None], prolong_t, bucket, bucket_count
    ).reshape(owner_count, CAP_OWNER, block_size, block_size)
    arrived_diag = lax.all_to_all(outgoing_diag, "wide", split_axis=0, concat_axis=0, tiled=True)

    shard_blocks = lax.all_gather(prolong, "narrow", axis=0, tiled=True)
    piece_rows = shard_blocks.shape[0]
    off_cols = jnp.clip(a_cols[:, 1:], 0, piece_rows - 1).astype(jnp.int32)
    outgoing_off = galerkin_buckets(
        a_blocks, tuple(range(1, per_row)), shard_blocks, off_cols, prolong_t, bucket, bucket_count
    ).reshape(owner_count, CAP_OWNER * (per_row - 1), block_size, block_size)
    arrived_off = lax.all_to_all(outgoing_off, "wide", split_axis=0, concat_axis=0, tiled=True)

    slots_diag = arrived_slots[:, :, :1].reshape(-1)
    slots_off = arrived_slots[:, :, 1:].reshape(-1)
    slot_ids = jnp.arange(CB_DEV, dtype=jnp.int32)[:, None]
    coarse_sum = jnp.dot(
        (slot_ids == slots_diag[None, :]).astype(jnp.bfloat16),
        arrived_diag.reshape(-1, block_size * block_size),
        preferred_element_type=jnp.float32,
    ) + jnp.dot(
        (slot_ids == slots_off[None, :]).astype(jnp.bfloat16),
        arrived_off.reshape(-1, block_size * block_size),
        preferred_element_type=jnp.float32,
    )
    return coarse_sum.reshape(CB_DEV, block_size, block_size)


def solution(mesh):
    return jax.shard_map(
        per_device,
        mesh=mesh,
        in_specs=(
            P(("wide", "narrow"), None, None, None),
            P(("wide", "narrow"), None),
            P(("wide", "narrow"), None, None),
            P(("wide", "narrow")),
            P(("wide", "narrow"), None),
        ),
        out_specs=P(("wide", "narrow"), None, None),
        check_vma=False,
    )
```

```python
import functools

import jax
import jax.numpy as jnp
from jax import lax
from jax.experimental import pallas as pl
from jax.experimental.pallas import tpu as pltpu
from jax.sharding import PartitionSpec as P

CAP_OWNER = 2
CB_DEV = 24


ROWS_PER_STEP = 4


def galerkin_kernel(n_k, bucket_ref, cols_ref, *refs):
    a_refs = refs[:n_k]
    right_refs = refs[n_k:n_k + ROWS_PER_STEP * n_k]
    pt_ref = refs[n_k + ROWS_PER_STEP * n_k]
    out_ref = refs[n_k + ROWS_PER_STEP * n_k + 1]
    step = pl.program_id(0)

    @pl.when(step == 0)
    def _():
        out_ref[...] = jnp.zeros_like(out_ref)

    for i in range(ROWS_PER_STEP):
        bucket = bucket_ref[step * ROWS_PER_STEP + i]
        for k in range(n_k):
            product = jnp.dot(
                a_refs[k][i], right_refs[i * n_k + k][...], preferred_element_type=jnp.float32
            ).astype(jnp.bfloat16)
            galerkin = lax.dot_general(
                pt_ref[i], product, (((0,), (0,)), ((), ())), preferred_element_type=jnp.float32
            )
            out_ref[bucket, k] = galerkin.astype(jnp.bfloat16)


def galerkin_buckets(a_blocks, ks, table, cols, prolong, bucket, bucket_count):
    slab_rows, unused_k, block_size, unused_size = a_blocks.shape
    n_k = len(ks)
    squeezed = pl.Squeezed()
    a_specs = [
        pl.BlockSpec((ROWS_PER_STEP, squeezed, block_size, block_size),
                     functools.partial(lambda k, s, b, c: (s, k, 0, 0), k))
        for k in ks
    ]
    right_specs = [
        pl.BlockSpec((squeezed, block_size, block_size),
                     functools.partial(lambda i, j, s, b, c: (c[s * ROWS_PER_STEP + i, j], 0, 0), i, j))
        for i in range(ROWS_PER_STEP)
        for j in range(n_k)
    ]
    pt_spec = pl.BlockSpec((ROWS_PER_STEP, block_size, block_size), lambda s, b, c: (s, 0, 0))
    out_spec = pl.BlockSpec(
        (bucket_count, n_k, block_size, block_size), lambda s, b, c: (0, 0, 0, 0)
    )
    flops = 4 * slab_rows * n_k * block_size ** 3
    moved = 2 * block_size * block_size * (slab_rows * (2 * n_k + 1) + bucket_count * n_k)
    return pl.pallas_call(
        functools.partial(galerkin_kernel, n_k),
        out_shape=jax.ShapeDtypeStruct((bucket_count, n_k, block_size, block_size), jnp.bfloat16),
        grid_spec=pltpu.PrefetchScalarGridSpec(
            num_scalar_prefetch=2,
            grid=(slab_rows // ROWS_PER_STEP,),
            in_specs=a_specs + right_specs + [pt_spec],
            out_specs=out_spec,
        ),
        compiler_params=pltpu.CompilerParams(dimension_semantics=("arbitrary",)),
        cost_estimate=pl.CostEstimate(flops=flops, bytes_accessed=moved, transcendentals=0),
    )(bucket, cols, *([a_blocks] * n_k), *([table] * (ROWS_PER_STEP * n_k)), prolong)


def reduce_kernel(has_init, slot_ref, *refs):
    if has_init:
        init_ref, blocks_ref, out_ref = refs
        out_ref[...] = init_ref[...]
    else:
        blocks_ref, out_ref = refs
        out_ref[...] = jnp.zeros_like(out_ref)
    slot_count = out_ref.shape[0]

    def add_block(index, carry):
        slot = slot_ref[index]

        @pl.when((slot >= 0) & (slot < slot_count))
        def _():
            target = jnp.clip(slot, 0, slot_count - 1)
            out_ref[target] = out_ref[target] + blocks_ref[index].astype(jnp.float32)

        return carry

    lax.fori_loop(0, blocks_ref.shape[0], add_block, 0)


def reduce_by_slot(slot_of_block, blocks, init=None):
    block_count, block_size, unused_size = blocks.shape
    whole = lambda shape: pl.BlockSpec(shape, lambda i, s: (0,) * len(shape))
    out_shape = (CB_DEV, block_size, block_size)
    in_specs = [whole(blocks.shape)]
    operands = [blocks]
    if init is not None:
        in_specs = [whole(out_shape)] + in_specs
        operands = [init] + operands
    return pl.pallas_call(
        functools.partial(reduce_kernel, init is not None),
        out_shape=jax.ShapeDtypeStruct(out_shape, jnp.float32),
        grid_spec=pltpu.PrefetchScalarGridSpec(
            num_scalar_prefetch=1, grid=(1,), in_specs=in_specs, out_specs=whole(out_shape)
        ),
        cost_estimate=pl.CostEstimate(
            flops=block_count * block_size * block_size,
            bytes_accessed=blocks.size * 2 + 8 * CB_DEV * block_size * block_size,
            transcendentals=0,
        ),
    )(slot_of_block.astype(jnp.int32), *operands)


def per_device(a_blocks, a_cols, prolong, owners, slots):
    slab_rows, per_row, block_size, unused_size = a_blocks.shape
    owner_count = lax.axis_size("wide")
    bucket_count = owner_count * CAP_OWNER

    row_ids = jnp.arange(slab_rows, dtype=jnp.int32)
    same_owner = (owners[:, None] == owners[None, :]) & (row_ids[None, :] < row_ids[:, None])
    owner_position = jnp.sum(same_owner.astype(jnp.int32), axis=1)
    bucket = jnp.clip(owners * CAP_OWNER + owner_position, 0, bucket_count - 1).astype(jnp.int32)
    info = jnp.concatenate([owners[:, None], slots], axis=1).astype(jnp.int32)
    all_info = lax.all_gather(info, "wide", axis=0, tiled=False)
    src_owner = all_info[:, :, 0]
    src_slots = all_info[:, :, 1:]
    src_same = (src_owner[:, :, None] == src_owner[:, None, :]) & (
        row_ids[None, None, :] < row_ids[None, :, None]
    )
    src_position = jnp.sum(src_same.astype(jnp.int32), axis=2)
    src_bucket = jnp.clip(src_owner * CAP_OWNER + src_position, 0, bucket_count - 1)
    me = lax.axis_index("wide")
    wanted = me * CAP_OWNER + jnp.arange(CAP_OWNER, dtype=jnp.int32)
    picked = src_bucket[:, None, :] == wanted[None, :, None]
    arrived_slots = (
        jnp.sum(jnp.where(picked[:, :, :, None], src_slots[:, None, :, :] + 1, 0), axis=2) - 1
    )

    outgoing_diag = galerkin_buckets(
        a_blocks, (0,), prolong, row_ids[:, None], prolong, bucket, bucket_count
    ).reshape(owner_count, CAP_OWNER, block_size, block_size)
    arrived_diag = lax.all_to_all(outgoing_diag, "wide", split_axis=0, concat_axis=0, tiled=True)

    shard_blocks = lax.all_gather(prolong, "narrow", axis=0, tiled=True)
    piece_rows = shard_blocks.shape[0]
    off_cols = jnp.clip(a_cols[:, 1:], 0, piece_rows - 1).astype(jnp.int32)
    outgoing_off = galerkin_buckets(
        a_blocks, tuple(range(1, per_row)), shard_blocks, off_cols, prolong, bucket, bucket_count
    ).reshape(owner_count, CAP_OWNER * (per_row - 1), block_size, block_size)
    arrived_off = lax.all_to_all(outgoing_off, "wide", split_axis=0, concat_axis=0, tiled=True)

    coarse_diag = reduce_by_slot(
        arrived_slots[:, :, 0].reshape(-1), arrived_diag.reshape(-1, block_size, block_size)
    )
    coarse_sum = reduce_by_slot(
        arrived_slots[:, :, 1:].reshape(-1),
        arrived_off.reshape(-1, block_size, block_size),
        coarse_diag,
    )
    return coarse_sum.reshape(CB_DEV, block_size, block_size)


def solution(mesh):
    return jax.shard_map(
        per_device,
        mesh=mesh,
        in_specs=(
            P(("wide", "narrow"), None, None, None),
            P(("wide", "narrow"), None),
            P(("wide", "narrow"), None, None),
            P(("wide", "narrow")),
            P(("wide", "narrow"), None),
        ),
        out_specs=P(("wide", "narrow"), None, None),
        check_vma=False,
    )
```

```python
import functools

import jax
import jax.numpy as jnp
from jax import lax
from jax.experimental import pallas as pl
from jax.experimental.pallas import tpu as pltpu
from jax.sharding import PartitionSpec as P

CAP_OWNER = 2
CB_DEV = 24


ROWS_PER_STEP = 4


def galerkin_kernel(n_k, bucket_ref, cols_ref, *refs):
    a_refs = refs[:n_k]
    right_refs = refs[n_k:n_k + ROWS_PER_STEP * n_k]
    pt_ref = refs[n_k + ROWS_PER_STEP * n_k]
    out_ref = refs[n_k + ROWS_PER_STEP * n_k + 1]
    step = pl.program_id(0)

    @pl.when(step == 0)
    def _():
        out_ref[...] = jnp.zeros_like(out_ref)

    for i in range(ROWS_PER_STEP):
        bucket = bucket_ref[step * ROWS_PER_STEP + i]
        for k in range(n_k):
            product = jnp.dot(
                a_refs[k][i], right_refs[i * n_k + k][...], preferred_element_type=jnp.float32
            ).astype(jnp.bfloat16)
            galerkin = lax.dot_general(
                pt_ref[i], product, (((0,), (0,)), ((), ())), preferred_element_type=jnp.float32
            )
            out_ref[bucket, k] = galerkin.astype(jnp.bfloat16)


def galerkin_buckets(a_blocks, ks, table, cols, prolong, bucket, bucket_count):
    slab_rows, unused_k, block_size, unused_size = a_blocks.shape
    n_k = len(ks)
    squeezed = pl.Squeezed()
    a_specs = [
        pl.BlockSpec((ROWS_PER_STEP, squeezed, block_size, block_size),
                     functools.partial(lambda k, s, b, c: (s, k, 0, 0), k))
        for k in ks
    ]
    right_specs = [
        pl.BlockSpec((squeezed, block_size, block_size),
                     functools.partial(lambda i, j, s, b, c: (c[s * ROWS_PER_STEP + i, j], 0, 0), i, j))
        for i in range(ROWS_PER_STEP)
        for j in range(n_k)
    ]
    pt_spec = pl.BlockSpec((ROWS_PER_STEP, block_size, block_size), lambda s, b, c: (s, 0, 0))
    out_spec = pl.BlockSpec(
        (bucket_count, n_k, block_size, block_size), lambda s, b, c: (0, 0, 0, 0)
    )
    flops = 4 * slab_rows * n_k * block_size ** 3
    moved = 2 * block_size * block_size * (slab_rows * (2 * n_k + 1) + bucket_count * n_k)
    return pl.pallas_call(
        functools.partial(galerkin_kernel, n_k),
        out_shape=jax.ShapeDtypeStruct((bucket_count, n_k, block_size, block_size), jnp.bfloat16),
        grid_spec=pltpu.PrefetchScalarGridSpec(
            num_scalar_prefetch=2,
            grid=(slab_rows // ROWS_PER_STEP,),
            in_specs=a_specs + right_specs + [pt_spec],
            out_specs=out_spec,
        ),
        compiler_params=pltpu.CompilerParams(dimension_semantics=("arbitrary",)),
        cost_estimate=pl.CostEstimate(flops=flops, bytes_accessed=moved, transcendentals=0),
    )(bucket, cols, *([a_blocks] * n_k), *([table] * (ROWS_PER_STEP * n_k)), prolong)


def reduce_kernel(has_init, slot_ref, *refs):
    if has_init:
        init_ref, blocks_ref, out_ref = refs
        out_ref[...] = init_ref[...]
    else:
        blocks_ref, out_ref = refs
        out_ref[...] = jnp.zeros_like(out_ref)
    slot_count = out_ref.shape[0]

    def add_block(index, carry):
        slot = slot_ref[index]

        @pl.when((slot >= 0) & (slot < slot_count))
        def _():
            target = jnp.clip(slot, 0, slot_count - 1)
            out_ref[target] = out_ref[target] + blocks_ref[index].astype(jnp.float32)

        return carry

    lax.fori_loop(0, blocks_ref.shape[0], add_block, 0)


def reduce_by_slot(slot_of_block, blocks, init=None):
    block_count, block_size, unused_size = blocks.shape
    whole = lambda shape: pl.BlockSpec(shape, lambda i, s: (0,) * len(shape))
    out_shape = (CB_DEV, block_size, block_size)
    in_specs = [whole(blocks.shape)]
    operands = [blocks]
    if init is not None:
        in_specs = [whole(out_shape)] + in_specs
        operands = [init] + operands
    return pl.pallas_call(
        functools.partial(reduce_kernel, init is not None),
        out_shape=jax.ShapeDtypeStruct(out_shape, jnp.float32),
        grid_spec=pltpu.PrefetchScalarGridSpec(
            num_scalar_prefetch=1, grid=(1,), in_specs=in_specs, out_specs=whole(out_shape)
        ),
        cost_estimate=pl.CostEstimate(
            flops=block_count * block_size * block_size,
            bytes_accessed=blocks.size * 2 + 8 * CB_DEV * block_size * block_size,
            transcendentals=0,
        ),
    )(slot_of_block.astype(jnp.int32), *operands)


def per_device(a_blocks, a_cols, prolong, owners, slots):
    slab_rows, per_row, block_size, unused_size = a_blocks.shape
    owner_count = lax.axis_size("wide")
    bucket_count = owner_count * CAP_OWNER

    row_ids = jnp.arange(slab_rows, dtype=jnp.int32)
    same_owner = (owners[:, None] == owners[None, :]) & (row_ids[None, :] < row_ids[:, None])
    owner_position = jnp.sum(same_owner.astype(jnp.int32), axis=1)
    bucket = jnp.clip(owners * CAP_OWNER + owner_position, 0, bucket_count - 1).astype(jnp.int32)
    info = jnp.concatenate([owners[:, None], slots], axis=1).astype(jnp.int32)
    all_info = lax.all_gather(info, "wide", axis=0, tiled=False)
    src_owner = all_info[:, :, 0]
    src_slots = all_info[:, :, 1:]
    src_same = (src_owner[:, :, None] == src_owner[:, None, :]) & (
        row_ids[None, None, :] < row_ids[None, :, None]
    )
    src_position = jnp.sum(src_same.astype(jnp.int32), axis=2)
    src_bucket = jnp.clip(src_owner * CAP_OWNER + src_position, 0, bucket_count - 1)
    me = lax.axis_index("wide")
    wanted = me * CAP_OWNER + jnp.arange(CAP_OWNER, dtype=jnp.int32)
    picked = src_bucket[:, None, :] == wanted[None, :, None]
    arrived_slots = (
        jnp.sum(jnp.where(picked[:, :, :, None], src_slots[:, None, :, :] + 1, 0), axis=2) - 1
    )

    outgoing_diag = galerkin_buckets(
        a_blocks, (0,), prolong, row_ids[:, None], prolong, bucket, bucket_count
    ).reshape(owner_count, CAP_OWNER, block_size, block_size)
    arrived_diag = lax.all_to_all(outgoing_diag, "wide", split_axis=0, concat_axis=0, tiled=True)

    shard_blocks = lax.all_gather(prolong, "narrow", axis=0, tiled=True)
    piece_rows = shard_blocks.shape[0]
    off_cols = jnp.clip(a_cols[:, 1:], 0, piece_rows - 1).astype(jnp.int32)
    bucket_after_info = jnp.maximum(bucket, jnp.minimum(all_info[0, 0, 0], 0))
    outgoing_off = galerkin_buckets(
        a_blocks, tuple(range(1, per_row)), shard_blocks, off_cols, prolong, bucket_after_info, bucket_count
    ).reshape(owner_count, CAP_OWNER * (per_row - 1), block_size, block_size)
    arrived_off = lax.all_to_all(outgoing_off, "wide", split_axis=0, concat_axis=0, tiled=True)

    coarse_diag = reduce_by_slot(
        arrived_slots[:, :, 0].reshape(-1), arrived_diag.reshape(-1, block_size, block_size)
    )
    coarse_sum = reduce_by_slot(
        arrived_slots[:, :, 1:].reshape(-1),
        arrived_off.reshape(-1, block_size, block_size),
        coarse_diag,
    )
    return coarse_sum.reshape(CB_DEV, block_size, block_size)


def solution(mesh):
    return jax.shard_map(
        per_device,
        mesh=mesh,
        in_specs=(
            P(("wide", "narrow"), None, None, None),
            P(("wide", "narrow"), None),
            P(("wide", "narrow"), None, None),
            P(("wide", "narrow")),
            P(("wide", "narrow"), None),
        ),
        out_specs=P(("wide", "narrow"), None, None),
        check_vma=False,
    )
```

```python
import functools

import jax
import jax.numpy as jnp
from jax import lax
from jax.experimental import pallas as pl
from jax.experimental.pallas import tpu as pltpu
from jax.sharding import PartitionSpec as P

CAP_OWNER = 2
CB_DEV = 24


ROWS_PER_STEP = 4


def galerkin_kernel(n_k, bucket_ref, cols_ref, *refs):
    a_refs = refs[:n_k]
    right_refs = refs[n_k:n_k + ROWS_PER_STEP * n_k]
    pt_ref = refs[n_k + ROWS_PER_STEP * n_k]
    out_ref = refs[n_k + ROWS_PER_STEP * n_k + 1]
    step = pl.program_id(0)

    @pl.when(step == 0)
    def _():
        out_ref[...] = jnp.zeros_like(out_ref)

    for i in range(ROWS_PER_STEP):
        bucket = bucket_ref[step * ROWS_PER_STEP + i]
        for k in range(n_k):
            product = jnp.dot(
                a_refs[k][i], right_refs[i * n_k + k][...], preferred_element_type=jnp.float32
            ).astype(jnp.bfloat16)
            galerkin = lax.dot_general(
                pt_ref[i], product, (((0,), (0,)), ((), ())), preferred_element_type=jnp.float32
            )
            out_ref[bucket, k] = galerkin.astype(jnp.bfloat16)


def galerkin_buckets(a_blocks, ks, table, cols, prolong, bucket, bucket_count):
    slab_rows, unused_k, block_size, unused_size = a_blocks.shape
    n_k = len(ks)
    squeezed = pl.Squeezed()
    a_specs = [
        pl.BlockSpec((ROWS_PER_STEP, squeezed, block_size, block_size),
                     functools.partial(lambda k, s, b, c: (s, k, 0, 0), k))
        for k in ks
    ]
    right_specs = [
        pl.BlockSpec((squeezed, block_size, block_size),
                     functools.partial(lambda i, j, s, b, c: (c[s * ROWS_PER_STEP + i, j], 0, 0), i, j))
        for i in range(ROWS_PER_STEP)
        for j in range(n_k)
    ]
    pt_spec = pl.BlockSpec((ROWS_PER_STEP, block_size, block_size), lambda s, b, c: (s, 0, 0))
    out_spec = pl.BlockSpec(
        (bucket_count, n_k, block_size, block_size), lambda s, b, c: (0, 0, 0, 0)
    )
    flops = 4 * slab_rows * n_k * block_size ** 3
    moved = 2 * block_size * block_size * (slab_rows * (2 * n_k + 1) + bucket_count * n_k)
    return pl.pallas_call(
        functools.partial(galerkin_kernel, n_k),
        out_shape=jax.ShapeDtypeStruct((bucket_count, n_k, block_size, block_size), jnp.bfloat16),
        grid_spec=pltpu.PrefetchScalarGridSpec(
            num_scalar_prefetch=2,
            grid=(slab_rows // ROWS_PER_STEP,),
            in_specs=a_specs + right_specs + [pt_spec],
            out_specs=out_spec,
        ),
        compiler_params=pltpu.CompilerParams(dimension_semantics=("arbitrary",)),
        cost_estimate=pl.CostEstimate(flops=flops, bytes_accessed=moved, transcendentals=0),
    )(bucket, cols, *([a_blocks] * n_k), *([table] * (ROWS_PER_STEP * n_k)), prolong)


def reduce_kernel(has_init, slot_ref, *refs):
    if has_init:
        init_ref, blocks_ref, out_ref = refs
        out_ref[...] = init_ref[...]
    else:
        blocks_ref, out_ref = refs
        out_ref[...] = jnp.zeros_like(out_ref)
    slot_count = out_ref.shape[0]

    def add_block(index, carry):
        slot = slot_ref[index]

        @pl.when((slot >= 0) & (slot < slot_count))
        def _():
            target = jnp.clip(slot, 0, slot_count - 1)
            out_ref[target] = out_ref[target] + blocks_ref[index].astype(jnp.float32)

        return carry

    lax.fori_loop(0, blocks_ref.shape[0], add_block, 0)


def reduce_by_slot(slot_of_block, blocks, init=None):
    block_count, block_size, unused_size = blocks.shape
    whole = lambda shape: pl.BlockSpec(shape, lambda i, s: (0,) * len(shape))
    out_shape = (CB_DEV, block_size, block_size)
    in_specs = [whole(blocks.shape)]
    operands = [blocks]
    if init is not None:
        in_specs = [whole(out_shape)] + in_specs
        operands = [init] + operands
    return pl.pallas_call(
        functools.partial(reduce_kernel, init is not None),
        out_shape=jax.ShapeDtypeStruct(out_shape, jnp.float32),
        grid_spec=pltpu.PrefetchScalarGridSpec(
            num_scalar_prefetch=1, grid=(1,), in_specs=in_specs, out_specs=whole(out_shape)
        ),
        cost_estimate=pl.CostEstimate(
            flops=block_count * block_size * block_size,
            bytes_accessed=blocks.size * 2 + 8 * CB_DEV * block_size * block_size,
            transcendentals=0,
        ),
    )(slot_of_block.astype(jnp.int32), *operands)


def per_device(a_blocks, a_cols, prolong, owners, slots):
    slab_rows, per_row, block_size, unused_size = a_blocks.shape
    owner_count = lax.axis_size("wide")
    bucket_count = owner_count * CAP_OWNER

    row_ids = jnp.arange(slab_rows, dtype=jnp.int32)
    same_owner = (owners[:, None] == owners[None, :]) & (row_ids[None, :] < row_ids[:, None])
    owner_position = jnp.sum(same_owner.astype(jnp.int32), axis=1)
    bucket = jnp.clip(owners * CAP_OWNER + owner_position, 0, bucket_count - 1).astype(jnp.int32)
    bucket_map = jnp.arange(bucket_count, dtype=jnp.int32)[:, None] == bucket[None, :]
    outgoing_slots = (
        jnp.sum(jnp.where(bucket_map[:, :, None], slots[None, :, :] + 1, 0), axis=1) - 1
    )
    outgoing_slots = outgoing_slots.reshape(owner_count, CAP_OWNER, per_row)
    arrived_slots = lax.all_to_all(outgoing_slots, "wide", split_axis=0, concat_axis=0, tiled=True)

    outgoing_diag = galerkin_buckets(
        a_blocks, (0,), prolong, row_ids[:, None], prolong, bucket, bucket_count
    ).reshape(owner_count, CAP_OWNER, block_size, block_size)
    arrived_diag = lax.all_to_all(outgoing_diag, "wide", split_axis=0, concat_axis=0, tiled=True)

    shard_blocks = lax.all_gather(prolong, "narrow", axis=0, tiled=True)
    piece_rows = shard_blocks.shape[0]
    off_cols = jnp.clip(a_cols[:, 1:], 0, piece_rows - 1).astype(jnp.int32)
    outgoing_off = galerkin_buckets(
        a_blocks, tuple(range(1, per_row)), shard_blocks, off_cols, prolong, bucket, bucket_count
    ).reshape(owner_count, CAP_OWNER * (per_row - 1), block_size, block_size)
    arrived_off = lax.all_to_all(outgoing_off, "wide", split_axis=0, concat_axis=0, tiled=True)

    coarse_diag = reduce_by_slot(
        arrived_slots[:, :, 0].reshape(-1), arrived_diag.reshape(-1, block_size, block_size)
    )
    coarse_sum = reduce_by_slot(
        arrived_slots[:, :, 1:].reshape(-1),
        arrived_off.reshape(-1, block_size, block_size),
        coarse_diag,
    )
    return coarse_sum.reshape(CB_DEV, block_size, block_size)


def solution(mesh):
    return jax.shard_map(
        per_device,
        mesh=mesh,
        in_specs=(
            P(("wide", "narrow"), None, None, None),
            P(("wide", "narrow"), None),
            P(("wide", "narrow"), None, None),
            P(("wide", "narrow")),
            P(("wide", "narrow"), None),
        ),
        out_specs=P(("wide", "narrow"), None, None),
        check_vma=False,
    )
```

```python
import functools

import jax
import jax.numpy as jnp
from jax import lax
from jax.experimental import pallas as pl
from jax.experimental.pallas import tpu as pltpu
from jax.sharding import PartitionSpec as P

CAP_OWNER = 2
CB_DEV = 24


ROWS_PER_STEP = 4


def galerkin_kernel(n_k, bucket_ref, cols_ref, *refs):
    a_refs = refs[:n_k]
    right_refs = refs[n_k:n_k + ROWS_PER_STEP * n_k]
    pt_ref = refs[n_k + ROWS_PER_STEP * n_k]
    out_ref = refs[n_k + ROWS_PER_STEP * n_k + 1]
    step = pl.program_id(0)

    @pl.when(step == 0)
    def _():
        out_ref[...] = jnp.zeros_like(out_ref)

    for i in range(ROWS_PER_STEP):
        bucket = bucket_ref[step * ROWS_PER_STEP + i]
        for k in range(n_k):
            product = jnp.dot(
                a_refs[k][i], right_refs[i * n_k + k][...], preferred_element_type=jnp.float32
            ).astype(jnp.bfloat16)
            galerkin = lax.dot_general(
                pt_ref[i], product, (((0,), (0,)), ((), ())), preferred_element_type=jnp.float32
            )
            out_ref[bucket, k] = galerkin.astype(jnp.bfloat16)


META_ROWS = 16


def diag_kernel(bucket_ref, slot_ref, a_ref, p_ref, out_ref):
    step = pl.program_id(0)
    block_size = p_ref.shape[-1]
    per_row = slot_ref.shape[1]

    @pl.when(step == 0)
    def _():
        out_ref[...] = jnp.zeros_like(out_ref)

    rows = lax.broadcasted_iota(jnp.int32, (META_ROWS, block_size), 0)
    cols = lax.broadcasted_iota(jnp.int32, (META_ROWS, block_size), 1)
    for i in range(ROWS_PER_STEP):
        row = step * ROWS_PER_STEP + i
        bucket = bucket_ref[row]
        owner = bucket // CAP_OWNER
        pos = bucket - owner * CAP_OWNER
        product = jnp.dot(a_ref[i], p_ref[i], preferred_element_type=jnp.float32).astype(jnp.bfloat16)
        galerkin = lax.dot_general(
            p_ref[i], product, (((0,), (0,)), ((), ())), preferred_element_type=jnp.float32
        )
        out_ref[owner, pl.ds(pl.multiple_of(pos * block_size, block_size), block_size), :] = (
            galerkin.astype(jnp.bfloat16)
        )
        meta = jnp.zeros((META_ROWS, block_size), jnp.int32)
        for k in range(per_row):
            meta = jnp.where((rows == 0) & (cols == pos * per_row + k), slot_ref[row, k] + 1, meta)
        meta_rows = pl.ds(CAP_OWNER * block_size, META_ROWS)
        out_ref[owner, meta_rows, :] = (
            out_ref[owner, meta_rows, :].astype(jnp.float32) + meta.astype(jnp.float32)
        ).astype(jnp.bfloat16)


def diag_buckets(a_blocks, prolong, slots, bucket, owner_count):
    slab_rows, per_row, block_size, unused_size = a_blocks.shape
    squeezed = pl.Squeezed()
    chunk_rows = CAP_OWNER * block_size + META_ROWS
    return pl.pallas_call(
        diag_kernel,
        out_shape=jax.ShapeDtypeStruct((owner_count, chunk_rows, block_size), jnp.bfloat16),
        grid_spec=pltpu.PrefetchScalarGridSpec(
            num_scalar_prefetch=2,
            grid=(slab_rows // ROWS_PER_STEP,),
            in_specs=[
                pl.BlockSpec((ROWS_PER_STEP, squeezed, block_size, block_size), lambda s, b, c: (s, 0, 0, 0)),
                pl.BlockSpec((ROWS_PER_STEP, block_size, block_size), lambda s, b, c: (s, 0, 0)),
            ],
            out_specs=pl.BlockSpec((owner_count, chunk_rows, block_size), lambda s, b, c: (0, 0, 0)),
        ),
        compiler_params=pltpu.CompilerParams(dimension_semantics=("arbitrary",)),
        cost_estimate=pl.CostEstimate(
            flops=4 * slab_rows * block_size ** 3,
            bytes_accessed=2 * block_size * (2 * slab_rows * block_size + owner_count * chunk_rows),
            transcendentals=0,
        ),
    )(bucket, slots.astype(jnp.int32), a_blocks, prolong)


def galerkin_buckets(a_blocks, ks, table, cols, prolong, bucket, bucket_count):
    slab_rows, unused_k, block_size, unused_size = a_blocks.shape
    n_k = len(ks)
    squeezed = pl.Squeezed()
    a_specs = [
        pl.BlockSpec((ROWS_PER_STEP, squeezed, block_size, block_size),
                     functools.partial(lambda k, s, b, c: (s, k, 0, 0), k))
        for k in ks
    ]
    right_specs = [
        pl.BlockSpec((squeezed, block_size, block_size),
                     functools.partial(lambda i, j, s, b, c: (c[s * ROWS_PER_STEP + i, j], 0, 0), i, j))
        for i in range(ROWS_PER_STEP)
        for j in range(n_k)
    ]
    pt_spec = pl.BlockSpec((ROWS_PER_STEP, block_size, block_size), lambda s, b, c: (s, 0, 0))
    out_spec = pl.BlockSpec(
        (bucket_count, n_k, block_size, block_size), lambda s, b, c: (0, 0, 0, 0)
    )
    flops = 4 * slab_rows * n_k * block_size ** 3
    moved = 2 * block_size * block_size * (slab_rows * (2 * n_k + 1) + bucket_count * n_k)
    return pl.pallas_call(
        functools.partial(galerkin_kernel, n_k),
        out_shape=jax.ShapeDtypeStruct((bucket_count, n_k, block_size, block_size), jnp.bfloat16),
        grid_spec=pltpu.PrefetchScalarGridSpec(
            num_scalar_prefetch=2,
            grid=(slab_rows // ROWS_PER_STEP,),
            in_specs=a_specs + right_specs + [pt_spec],
            out_specs=out_spec,
        ),
        compiler_params=pltpu.CompilerParams(dimension_semantics=("arbitrary",)),
        cost_estimate=pl.CostEstimate(flops=flops, bytes_accessed=moved, transcendentals=0),
    )(bucket, cols, *([a_blocks] * n_k), *([table] * (ROWS_PER_STEP * n_k)), prolong)


def reduce_kernel(has_init, slot_ref, *refs):
    if has_init:
        init_ref, blocks_ref, out_ref = refs
        out_ref[...] = init_ref[...]
    else:
        blocks_ref, out_ref = refs
        out_ref[...] = jnp.zeros_like(out_ref)
    slot_count = out_ref.shape[0]

    def add_block(index, carry):
        slot = slot_ref[index]

        @pl.when((slot >= 0) & (slot < slot_count))
        def _():
            target = jnp.clip(slot, 0, slot_count - 1)
            out_ref[target] = out_ref[target] + blocks_ref[index].astype(jnp.float32)

        return carry

    lax.fori_loop(0, blocks_ref.shape[0], add_block, 0)


def reduce_by_slot(slot_of_block, blocks, init=None):
    block_count, block_size, unused_size = blocks.shape
    whole = lambda shape: pl.BlockSpec(shape, lambda i, s: (0,) * len(shape))
    out_shape = (CB_DEV, block_size, block_size)
    in_specs = [whole(blocks.shape)]
    operands = [blocks]
    if init is not None:
        in_specs = [whole(out_shape)] + in_specs
        operands = [init] + operands
    return pl.pallas_call(
        functools.partial(reduce_kernel, init is not None),
        out_shape=jax.ShapeDtypeStruct(out_shape, jnp.float32),
        grid_spec=pltpu.PrefetchScalarGridSpec(
            num_scalar_prefetch=1, grid=(1,), in_specs=in_specs, out_specs=whole(out_shape)
        ),
        cost_estimate=pl.CostEstimate(
            flops=block_count * block_size * block_size,
            bytes_accessed=blocks.size * 2 + 8 * CB_DEV * block_size * block_size,
            transcendentals=0,
        ),
    )(slot_of_block.astype(jnp.int32), *operands)


def per_device(a_blocks, a_cols, prolong, owners, slots):
    slab_rows, per_row, block_size, unused_size = a_blocks.shape
    owner_count = lax.axis_size("wide")
    bucket_count = owner_count * CAP_OWNER

    row_ids = jnp.arange(slab_rows, dtype=jnp.int32)
    same_owner = (owners[:, None] == owners[None, :]) & (row_ids[None, :] < row_ids[:, None])
    owner_position = jnp.sum(same_owner.astype(jnp.int32), axis=1)
    bucket = jnp.clip(owners * CAP_OWNER + owner_position, 0, bucket_count - 1).astype(jnp.int32)
    outgoing_diag = diag_buckets(a_blocks, prolong, slots, bucket, owner_count)
    arrived_diag = lax.all_to_all(outgoing_diag, "wide", split_axis=0, concat_axis=0, tiled=True)
    arrived_meta = arrived_diag[:, CAP_OWNER * block_size, : CAP_OWNER * per_row].astype(jnp.float32)
    arrived_slots = (jnp.round(arrived_meta).astype(jnp.int32) - 1).reshape(
        owner_count, CAP_OWNER, per_row
    )

    shard_blocks = lax.all_gather(prolong, "narrow", axis=0, tiled=True)
    piece_rows = shard_blocks.shape[0]
    off_cols = jnp.clip(a_cols[:, 1:], 0, piece_rows - 1).astype(jnp.int32)
    outgoing_off = galerkin_buckets(
        a_blocks, tuple(range(1, per_row)), shard_blocks, off_cols, prolong, bucket, bucket_count
    ).reshape(owner_count, CAP_OWNER * (per_row - 1), block_size, block_size)
    arrived_off = lax.all_to_all(outgoing_off, "wide", split_axis=0, concat_axis=0, tiled=True)

    coarse_diag = reduce_by_slot(
        arrived_slots[:, :, 0].reshape(-1),
        arrived_diag[:, : CAP_OWNER * block_size].reshape(-1, block_size, block_size),
    )
    coarse_sum = reduce_by_slot(
        arrived_slots[:, :, 1:].reshape(-1),
        arrived_off.reshape(-1, block_size, block_size),
        coarse_diag,
    )
    return coarse_sum.reshape(CB_DEV, block_size, block_size)


def solution(mesh):
    return jax.shard_map(
        per_device,
        mesh=mesh,
        in_specs=(
            P(("wide", "narrow"), None, None, None),
            P(("wide", "narrow"), None),
            P(("wide", "narrow"), None, None),
            P(("wide", "narrow")),
            P(("wide", "narrow"), None),
        ),
        out_specs=P(("wide", "narrow"), None, None),
        check_vma=False,
    )
```

```python
import functools

import jax
import jax.numpy as jnp
from jax import lax
from jax.experimental import pallas as pl
from jax.experimental.pallas import tpu as pltpu
from jax.sharding import PartitionSpec as P

CAP_OWNER = 2
CB_DEV = 24


ROWS_PER_STEP = 4


def galerkin_kernel(n_k, bucket_ref, cols_ref, *refs):
    a_refs = refs[:n_k]
    right_refs = refs[n_k:n_k + ROWS_PER_STEP * n_k]
    pt_ref = refs[n_k + ROWS_PER_STEP * n_k]
    out_ref = refs[n_k + ROWS_PER_STEP * n_k + 1]
    step = pl.program_id(0)

    @pl.when(step == 0)
    def _():
        out_ref[...] = jnp.zeros_like(out_ref)

    for i in range(ROWS_PER_STEP):
        bucket = bucket_ref[step * ROWS_PER_STEP + i]
        for k in range(n_k):
            product = jnp.dot(
                a_refs[k][i], right_refs[i * n_k + k][...], preferred_element_type=jnp.float32
            ).astype(jnp.bfloat16)
            galerkin = lax.dot_general(
                pt_ref[i], product, (((0,), (0,)), ((), ())), preferred_element_type=jnp.float32
            )
            out_ref[bucket, k] = galerkin.astype(jnp.bfloat16)


META_ROWS = 16


def diag_kernel(per_row, bucket_ref, slot_ref, a_ref, p_ref, out_ref):
    step = pl.program_id(0)
    block_size = p_ref.shape[-1]

    @pl.when(step == 0)
    def _():
        out_ref[...] = jnp.zeros_like(out_ref)

    rows = lax.broadcasted_iota(jnp.int32, (META_ROWS, block_size), 0)
    cols = lax.broadcasted_iota(jnp.int32, (META_ROWS, block_size), 1)
    for i in range(ROWS_PER_STEP):
        row = step * ROWS_PER_STEP + i
        bucket = bucket_ref[row]
        owner = bucket // CAP_OWNER
        pos = bucket - owner * CAP_OWNER
        product = jnp.dot(a_ref[i], p_ref[i], preferred_element_type=jnp.float32).astype(jnp.bfloat16)
        galerkin = lax.dot_general(
            p_ref[i], product, (((0,), (0,)), ((), ())), preferred_element_type=jnp.float32
        )
        out_ref[owner, pl.ds(pl.multiple_of(pos * block_size, block_size), block_size), :] = (
            galerkin.astype(jnp.bfloat16)
        )
        meta = jnp.zeros((META_ROWS, block_size), jnp.int32)
        for k in range(per_row):
            meta = jnp.where((rows == 0) & (cols == pos * per_row + k), slot_ref[row, k] + 1, meta)
        meta_rows = pl.ds(CAP_OWNER * block_size, META_ROWS)
        out_ref[owner, meta_rows, :] = (
            out_ref[owner, meta_rows, :].astype(jnp.float32) + meta.astype(jnp.float32)
        ).astype(jnp.bfloat16)


def diag_buckets(a_blocks, prolong, slots, bucket, owner_count):
    slab_rows, per_row, block_size, unused_size = a_blocks.shape
    squeezed = pl.Squeezed()
    chunk_rows = CAP_OWNER * block_size + META_ROWS
    return pl.pallas_call(
        functools.partial(diag_kernel, per_row),
        out_shape=jax.ShapeDtypeStruct((owner_count, chunk_rows, block_size), jnp.bfloat16),
        grid_spec=pltpu.PrefetchScalarGridSpec(
            num_scalar_prefetch=2,
            grid=(slab_rows // ROWS_PER_STEP,),
            in_specs=[
                pl.BlockSpec((ROWS_PER_STEP, squeezed, block_size, block_size), lambda s, b, c: (s, 0, 0, 0)),
                pl.BlockSpec((ROWS_PER_STEP, block_size, block_size), lambda s, b, c: (s, 0, 0)),
            ],
            out_specs=pl.BlockSpec((owner_count, chunk_rows, block_size), lambda s, b, c: (0, 0, 0)),
        ),
        compiler_params=pltpu.CompilerParams(dimension_semantics=("arbitrary",)),
        cost_estimate=pl.CostEstimate(
            flops=4 * slab_rows * block_size ** 3,
            bytes_accessed=2 * block_size * (2 * slab_rows * block_size + owner_count * chunk_rows),
            transcendentals=0,
        ),
    )(bucket, slots.astype(jnp.int32), a_blocks, prolong)


def galerkin_buckets(a_blocks, ks, table, cols, prolong, bucket, bucket_count):
    slab_rows, unused_k, block_size, unused_size = a_blocks.shape
    n_k = len(ks)
    squeezed = pl.Squeezed()
    a_specs = [
        pl.BlockSpec((ROWS_PER_STEP, squeezed, block_size, block_size),
                     functools.partial(lambda k, s, b, c: (s, k, 0, 0), k))
        for k in ks
    ]
    right_specs = [
        pl.BlockSpec((squeezed, block_size, block_size),
                     functools.partial(lambda i, j, s, b, c: (c[s * ROWS_PER_STEP + i, j], 0, 0), i, j))
        for i in range(ROWS_PER_STEP)
        for j in range(n_k)
    ]
    pt_spec = pl.BlockSpec((ROWS_PER_STEP, block_size, block_size), lambda s, b, c: (s, 0, 0))
    out_spec = pl.BlockSpec(
        (bucket_count, n_k, block_size, block_size), lambda s, b, c: (0, 0, 0, 0)
    )
    flops = 4 * slab_rows * n_k * block_size ** 3
    moved = 2 * block_size * block_size * (slab_rows * (2 * n_k + 1) + bucket_count * n_k)
    return pl.pallas_call(
        functools.partial(galerkin_kernel, n_k),
        out_shape=jax.ShapeDtypeStruct((bucket_count, n_k, block_size, block_size), jnp.bfloat16),
        grid_spec=pltpu.PrefetchScalarGridSpec(
            num_scalar_prefetch=2,
            grid=(slab_rows // ROWS_PER_STEP,),
            in_specs=a_specs + right_specs + [pt_spec],
            out_specs=out_spec,
        ),
        compiler_params=pltpu.CompilerParams(dimension_semantics=("arbitrary",)),
        cost_estimate=pl.CostEstimate(flops=flops, bytes_accessed=moved, transcendentals=0),
    )(bucket, cols, *([a_blocks] * n_k), *([table] * (ROWS_PER_STEP * n_k)), prolong)


REDUCE_CHUNK = 16


def reduce_kernel(has_init, slot_ref, *refs):
    if has_init:
        init_ref, blocks_ref, out_ref = refs
    else:
        blocks_ref, out_ref = refs
    step = pl.program_id(0)
    slot_count = out_ref.shape[0]

    @pl.when(step == 0)
    def _():
        if has_init:
            out_ref[...] = init_ref[...]
        else:
            out_ref[...] = jnp.zeros_like(out_ref)

    def add_block(index, carry):
        slot = slot_ref[step * REDUCE_CHUNK + index]

        @pl.when((slot >= 0) & (slot < slot_count))
        def _():
            target = jnp.clip(slot, 0, slot_count - 1)
            out_ref[target] = out_ref[target] + blocks_ref[index].astype(jnp.float32)

        return carry

    lax.fori_loop(0, REDUCE_CHUNK, add_block, 0)


def reduce_by_slot(slot_of_block, blocks, init=None):
    block_count, block_size, unused_size = blocks.shape
    out_shape = (CB_DEV, block_size, block_size)
    whole = pl.BlockSpec(out_shape, lambda i, s: (0, 0, 0))
    in_specs = [pl.BlockSpec((REDUCE_CHUNK, block_size, block_size), lambda i, s: (i, 0, 0))]
    operands = [blocks]
    if init is not None:
        in_specs = [whole] + in_specs
        operands = [init] + operands
    return pl.pallas_call(
        functools.partial(reduce_kernel, init is not None),
        out_shape=jax.ShapeDtypeStruct(out_shape, jnp.float32),
        grid_spec=pltpu.PrefetchScalarGridSpec(
            num_scalar_prefetch=1,
            grid=(block_count // REDUCE_CHUNK,),
            in_specs=in_specs,
            out_specs=whole,
        ),
        compiler_params=pltpu.CompilerParams(dimension_semantics=("arbitrary",)),
        cost_estimate=pl.CostEstimate(
            flops=block_count * block_size * block_size,
            bytes_accessed=blocks.size * 2 + 8 * CB_DEV * block_size * block_size,
            transcendentals=0,
        ),
    )(slot_of_block.astype(jnp.int32), *operands)


def per_device(a_blocks, a_cols, prolong, owners, slots):
    slab_rows, per_row, block_size, unused_size = a_blocks.shape
    owner_count = lax.axis_size("wide")
    bucket_count = owner_count * CAP_OWNER

    row_ids = jnp.arange(slab_rows, dtype=jnp.int32)
    same_owner = (owners[:, None] == owners[None, :]) & (row_ids[None, :] < row_ids[:, None])
    owner_position = jnp.sum(same_owner.astype(jnp.int32), axis=1)
    bucket = jnp.clip(owners * CAP_OWNER + owner_position, 0, bucket_count - 1).astype(jnp.int32)
    outgoing_diag = diag_buckets(a_blocks, prolong, slots, bucket, owner_count)
    arrived_diag = lax.all_to_all(outgoing_diag, "wide", split_axis=0, concat_axis=0, tiled=True)
    arrived_meta = arrived_diag[:, CAP_OWNER * block_size, : CAP_OWNER * per_row].astype(jnp.float32)
    arrived_slots = (jnp.round(arrived_meta).astype(jnp.int32) - 1).reshape(
        owner_count, CAP_OWNER, per_row
    )

    shard_blocks = lax.all_gather(prolong, "narrow", axis=0, tiled=True)
    piece_rows = shard_blocks.shape[0]
    off_cols = jnp.clip(a_cols[:, 1:], 0, piece_rows - 1).astype(jnp.int32)
    outgoing_off = galerkin_buckets(
        a_blocks, tuple(range(1, per_row)), shard_blocks, off_cols, prolong, bucket, bucket_count
    ).reshape(owner_count, CAP_OWNER * (per_row - 1), block_size, block_size)
    arrived_off = lax.all_to_all(outgoing_off, "wide", split_axis=0, concat_axis=0, tiled=True)

    coarse_diag = reduce_by_slot(
        arrived_slots[:, :, 0].reshape(-1),
        arrived_diag[:, : CAP_OWNER * block_size].reshape(-1, block_size, block_size),
    )
    coarse_sum = reduce_by_slot(
        arrived_slots[:, :, 1:].reshape(-1),
        arrived_off.reshape(-1, block_size, block_size),
        coarse_diag,
    )
    return coarse_sum.reshape(CB_DEV, block_size, block_size)


def solution(mesh):
    return jax.shard_map(
        per_device,
        mesh=mesh,
        in_specs=(
            P(("wide", "narrow"), None, None, None),
            P(("wide", "narrow"), None),
            P(("wide", "narrow"), None, None),
            P(("wide", "narrow")),
            P(("wide", "narrow"), None),
        ),
        out_specs=P(("wide", "narrow"), None, None),
        check_vma=False,
    )
```

```python
import functools

import jax
import jax.numpy as jnp
from jax import lax
from jax.experimental import pallas as pl
from jax.experimental.pallas import tpu as pltpu
from jax.sharding import PartitionSpec as P

CAP_OWNER = 2
CB_DEV = 24


ROWS_PER_STEP = 8


def galerkin_kernel(n_k, bucket_ref, cols_ref, *refs):
    a_refs = refs[:n_k]
    right_refs = refs[n_k:n_k + ROWS_PER_STEP * n_k]
    pt_ref = refs[n_k + ROWS_PER_STEP * n_k]
    out_ref = refs[n_k + ROWS_PER_STEP * n_k + 1]
    step = pl.program_id(0)

    @pl.when(step == 0)
    def _():
        out_ref[...] = jnp.zeros_like(out_ref)

    for i in range(ROWS_PER_STEP):
        bucket = bucket_ref[step * ROWS_PER_STEP + i]
        for k in range(n_k):
            product = jnp.dot(
                a_refs[k][i], right_refs[i * n_k + k][...], preferred_element_type=jnp.float32
            ).astype(jnp.bfloat16)
            galerkin = lax.dot_general(
                pt_ref[i], product, (((0,), (0,)), ((), ())), preferred_element_type=jnp.float32
            )
            out_ref[bucket, k] = galerkin.astype(jnp.bfloat16)


META_ROWS = 16


def diag_kernel(bucket_ref, slot_ref, a_ref, p_ref, out_ref):
    step = pl.program_id(0)
    block_size = p_ref.shape[-1]
    per_row = slot_ref.shape[1]

    @pl.when(step == 0)
    def _():
        out_ref[...] = jnp.zeros_like(out_ref)

    rows = lax.broadcasted_iota(jnp.int32, (META_ROWS, block_size), 0)
    cols = lax.broadcasted_iota(jnp.int32, (META_ROWS, block_size), 1)
    for i in range(ROWS_PER_STEP):
        row = step * ROWS_PER_STEP + i
        bucket = bucket_ref[row]
        owner = bucket // CAP_OWNER
        pos = bucket - owner * CAP_OWNER
        product = jnp.dot(a_ref[i], p_ref[i], preferred_element_type=jnp.float32).astype(jnp.bfloat16)
        galerkin = lax.dot_general(
            p_ref[i], product, (((0,), (0,)), ((), ())), preferred_element_type=jnp.float32
        )
        out_ref[owner, pl.ds(pl.multiple_of(pos * block_size, block_size), block_size), :] = (
            galerkin.astype(jnp.bfloat16)
        )
        meta = jnp.zeros((META_ROWS, block_size), jnp.int32)
        for k in range(per_row):
            meta = jnp.where((rows == 0) & (cols == pos * per_row + k), slot_ref[row, k] + 1, meta)
        meta_rows = pl.ds(CAP_OWNER * block_size, META_ROWS)
        out_ref[owner, meta_rows, :] = (
            out_ref[owner, meta_rows, :].astype(jnp.float32) + meta.astype(jnp.float32)
        ).astype(jnp.bfloat16)


def diag_buckets(a_blocks, prolong, slots, bucket, owner_count):
    slab_rows, per_row, block_size, unused_size = a_blocks.shape
    squeezed = pl.Squeezed()
    chunk_rows = CAP_OWNER * block_size + META_ROWS
    return pl.pallas_call(
        diag_kernel,
        out_shape=jax.ShapeDtypeStruct((owner_count, chunk_rows, block_size), jnp.bfloat16),
        grid_spec=pltpu.PrefetchScalarGridSpec(
            num_scalar_prefetch=2,
            grid=(slab_rows // ROWS_PER_STEP,),
            in_specs=[
                pl.BlockSpec((ROWS_PER_STEP, squeezed, block_size, block_size), lambda s, b, c: (s, 0, 0, 0)),
                pl.BlockSpec((ROWS_PER_STEP, block_size, block_size), lambda s, b, c: (s, 0, 0)),
            ],
            out_specs=pl.BlockSpec((owner_count, chunk_rows, block_size), lambda s, b, c: (0, 0, 0)),
        ),
        compiler_params=pltpu.CompilerParams(dimension_semantics=("arbitrary",)),
        cost_estimate=pl.CostEstimate(
            flops=4 * slab_rows * block_size ** 3,
            bytes_accessed=2 * block_size * (2 * slab_rows * block_size + owner_count * chunk_rows),
            transcendentals=0,
        ),
    )(bucket, slots.astype(jnp.int32), a_blocks, prolong)


def galerkin_buckets(a_blocks, ks, table, cols, prolong, bucket, bucket_count):
    slab_rows, unused_k, block_size, unused_size = a_blocks.shape
    n_k = len(ks)
    squeezed = pl.Squeezed()
    a_specs = [
        pl.BlockSpec((ROWS_PER_STEP, squeezed, block_size, block_size),
                     functools.partial(lambda k, s, b, c: (s, k, 0, 0), k))
        for k in ks
    ]
    right_specs = [
        pl.BlockSpec((squeezed, block_size, block_size),
                     functools.partial(lambda i, j, s, b, c: (c[s * ROWS_PER_STEP + i, j], 0, 0), i, j))
        for i in range(ROWS_PER_STEP)
        for j in range(n_k)
    ]
    pt_spec = pl.BlockSpec((ROWS_PER_STEP, block_size, block_size), lambda s, b, c: (s, 0, 0))
    out_spec = pl.BlockSpec(
        (bucket_count, n_k, block_size, block_size), lambda s, b, c: (0, 0, 0, 0)
    )
    flops = 4 * slab_rows * n_k * block_size ** 3
    moved = 2 * block_size * block_size * (slab_rows * (2 * n_k + 1) + bucket_count * n_k)
    return pl.pallas_call(
        functools.partial(galerkin_kernel, n_k),
        out_shape=jax.ShapeDtypeStruct((bucket_count, n_k, block_size, block_size), jnp.bfloat16),
        grid_spec=pltpu.PrefetchScalarGridSpec(
            num_scalar_prefetch=2,
            grid=(slab_rows // ROWS_PER_STEP,),
            in_specs=a_specs + right_specs + [pt_spec],
            out_specs=out_spec,
        ),
        compiler_params=pltpu.CompilerParams(dimension_semantics=("arbitrary",)),
        cost_estimate=pl.CostEstimate(flops=flops, bytes_accessed=moved, transcendentals=0),
    )(bucket, cols, *([a_blocks] * n_k), *([table] * (ROWS_PER_STEP * n_k)), prolong)


ACCUMULATORS = 4


def reduce_kernel(has_init, slot_ref, *refs):
    if has_init:
        init_ref, blocks_ref, out_ref = refs[:3]
    else:
        blocks_ref, out_ref = refs[:2]
    acc_refs = refs[-ACCUMULATORS:]
    slot_count = out_ref.shape[0]
    for acc_ref in acc_refs:
        acc_ref[...] = jnp.zeros_like(acc_ref)

    def add_blocks(index, carry):
        for j, acc_ref in enumerate(acc_refs):
            block = index * ACCUMULATORS + j
            slot = slot_ref[block]

            @pl.when((slot >= 0) & (slot < slot_count))
            def _():
                target = jnp.clip(slot, 0, slot_count - 1)
                acc_ref[target] = acc_ref[target] + blocks_ref[block].astype(jnp.float32)

        return carry

    lax.fori_loop(0, blocks_ref.shape[0] // ACCUMULATORS, add_blocks, 0)
    total = acc_refs[0][...]
    for acc_ref in acc_refs[1:]:
        total = total + acc_ref[...]
    if has_init:
        total = total + init_ref[...]
    out_ref[...] = total


def reduce_by_slot(slot_of_block, blocks, init=None):
    block_count, block_size, unused_size = blocks.shape
    whole = lambda shape: pl.BlockSpec(shape, lambda i, s: (0,) * len(shape))
    out_shape = (CB_DEV, block_size, block_size)
    in_specs = [whole(blocks.shape)]
    operands = [blocks]
    if init is not None:
        in_specs = [whole(out_shape)] + in_specs
        operands = [init] + operands
    return pl.pallas_call(
        functools.partial(reduce_kernel, init is not None),
        out_shape=jax.ShapeDtypeStruct(out_shape, jnp.float32),
        grid_spec=pltpu.PrefetchScalarGridSpec(
            num_scalar_prefetch=1,
            grid=(1,),
            in_specs=in_specs,
            out_specs=whole(out_shape),
            scratch_shapes=[pltpu.VMEM(out_shape, jnp.float32)] * ACCUMULATORS,
        ),
        cost_estimate=pl.CostEstimate(
            flops=block_count * block_size * block_size,
            bytes_accessed=blocks.size * 2 + 8 * CB_DEV * block_size * block_size,
            transcendentals=0,
        ),
    )(slot_of_block.astype(jnp.int32), *operands)


def per_device(a_blocks, a_cols, prolong, owners, slots):
    slab_rows, per_row, block_size, unused_size = a_blocks.shape
    owner_count = lax.axis_size("wide")
    bucket_count = owner_count * CAP_OWNER

    row_ids = jnp.arange(slab_rows, dtype=jnp.int32)
    same_owner = (owners[:, None] == owners[None, :]) & (row_ids[None, :] < row_ids[:, None])
    owner_position = jnp.sum(same_owner.astype(jnp.int32), axis=1)
    bucket = jnp.clip(owners * CAP_OWNER + owner_position, 0, bucket_count - 1).astype(jnp.int32)
    outgoing_diag = diag_buckets(a_blocks, prolong, slots, bucket, owner_count)
    arrived_diag = lax.all_to_all(outgoing_diag, "wide", split_axis=0, concat_axis=0, tiled=True)
    arrived_meta = arrived_diag[:, CAP_OWNER * block_size, : CAP_OWNER * per_row].astype(jnp.float32)
    arrived_slots = (jnp.round(arrived_meta).astype(jnp.int32) - 1).reshape(
        owner_count, CAP_OWNER, per_row
    )

    shard_blocks = lax.all_gather(prolong, "narrow", axis=0, tiled=True)
    piece_rows = shard_blocks.shape[0]
    off_cols = jnp.clip(a_cols[:, 1:], 0, piece_rows - 1).astype(jnp.int32)
    outgoing_off = galerkin_buckets(
        a_blocks, tuple(range(1, per_row)), shard_blocks, off_cols, prolong, bucket, bucket_count
    ).reshape(owner_count, CAP_OWNER * (per_row - 1), block_size, block_size)
    arrived_off = lax.all_to_all(outgoing_off, "wide", split_axis=0, concat_axis=0, tiled=True)

    coarse_diag = reduce_by_slot(
        arrived_slots[:, :, 0].reshape(-1),
        arrived_diag[:, : CAP_OWNER * block_size].reshape(-1, block_size, block_size),
    )
    coarse_sum = reduce_by_slot(
        arrived_slots[:, :, 1:].reshape(-1),
        arrived_off.reshape(-1, block_size, block_size),
        coarse_diag,
    )
    return coarse_sum.reshape(CB_DEV, block_size, block_size)


def solution(mesh):
    return jax.shard_map(
        per_device,
        mesh=mesh,
        in_specs=(
            P(("wide", "narrow"), None, None, None),
            P(("wide", "narrow"), None),
            P(("wide", "narrow"), None, None),
            P(("wide", "narrow")),
            P(("wide", "narrow"), None),
        ),
        out_specs=P(("wide", "narrow"), None, None),
        check_vma=False,
    )
```

```python
import functools

import jax
import jax.numpy as jnp
from jax import lax
from jax.experimental import pallas as pl
from jax.experimental.pallas import tpu as pltpu
from jax.sharding import PartitionSpec as P

CAP_OWNER = 2
CB_DEV = 24


ROWS_PER_STEP = 8


def galerkin_kernel(n_k, bucket_ref, cols_ref, *refs):
    a_refs = refs[:n_k]
    right_refs = refs[n_k:n_k + ROWS_PER_STEP * n_k]
    pt_ref = refs[n_k + ROWS_PER_STEP * n_k]
    out_ref = refs[n_k + ROWS_PER_STEP * n_k + 1]
    step = pl.program_id(0)

    @pl.when(step == 0)
    def _():
        out_ref[...] = jnp.zeros_like(out_ref)

    for i in range(ROWS_PER_STEP):
        bucket = bucket_ref[step * ROWS_PER_STEP + i]
        for k in range(n_k):
            product = jnp.dot(
                a_refs[k][i], right_refs[i * n_k + k][...], preferred_element_type=jnp.float32
            ).astype(jnp.bfloat16)
            galerkin = lax.dot_general(
                pt_ref[i], product, (((0,), (0,)), ((), ())), preferred_element_type=jnp.float32
            )
            out_ref[bucket, k] = galerkin.astype(jnp.bfloat16)


META_ROWS = 16


def diag_kernel(bucket_ref, slot_ref, a_ref, p_ref, out_ref):
    step = pl.program_id(0)
    block_size = p_ref.shape[-1]
    per_row = slot_ref.shape[1]

    @pl.when(step == 0)
    def _():
        out_ref[...] = jnp.zeros_like(out_ref)

    rows = lax.broadcasted_iota(jnp.int32, (META_ROWS, block_size), 0)
    cols = lax.broadcasted_iota(jnp.int32, (META_ROWS, block_size), 1)
    for i in range(ROWS_PER_STEP):
        row = step * ROWS_PER_STEP + i
        bucket = bucket_ref[row]
        owner = bucket // CAP_OWNER
        pos = bucket - owner * CAP_OWNER
        product = jnp.dot(a_ref[i], p_ref[i], preferred_element_type=jnp.float32).astype(jnp.bfloat16)
        galerkin = lax.dot_general(
            p_ref[i], product, (((0,), (0,)), ((), ())), preferred_element_type=jnp.float32
        )
        out_ref[owner, pl.ds(pl.multiple_of(pos * block_size, block_size), block_size), :] = (
            galerkin.astype(jnp.bfloat16)
        )
        meta = jnp.zeros((META_ROWS, block_size), jnp.int32)
        for k in range(per_row):
            meta = jnp.where((rows == 0) & (cols == pos * per_row + k), slot_ref[row, k] + 1, meta)
        meta_rows = pl.ds(CAP_OWNER * block_size, META_ROWS)
        out_ref[owner, meta_rows, :] = (
            out_ref[owner, meta_rows, :].astype(jnp.float32) + meta.astype(jnp.float32)
        ).astype(jnp.bfloat16)


def diag_buckets(a_blocks, prolong, slots, bucket, owner_count):
    slab_rows, per_row, block_size, unused_size = a_blocks.shape
    squeezed = pl.Squeezed()
    chunk_rows = CAP_OWNER * block_size + META_ROWS
    return pl.pallas_call(
        diag_kernel,
        out_shape=jax.ShapeDtypeStruct((owner_count, chunk_rows, block_size), jnp.bfloat16),
        grid_spec=pltpu.PrefetchScalarGridSpec(
            num_scalar_prefetch=2,
            grid=(slab_rows // ROWS_PER_STEP,),
            in_specs=[
                pl.BlockSpec((ROWS_PER_STEP, squeezed, block_size, block_size), lambda s, b, c: (s, 0, 0, 0)),
                pl.BlockSpec((ROWS_PER_STEP, block_size, block_size), lambda s, b, c: (s, 0, 0)),
            ],
            out_specs=pl.BlockSpec((owner_count, chunk_rows, block_size), lambda s, b, c: (0, 0, 0)),
        ),
        compiler_params=pltpu.CompilerParams(dimension_semantics=("arbitrary",)),
        cost_estimate=pl.CostEstimate(
            flops=4 * slab_rows * block_size ** 3,
            bytes_accessed=2 * block_size * (2 * slab_rows * block_size + owner_count * chunk_rows),
            transcendentals=0,
        ),
    )(bucket, slots.astype(jnp.int32), a_blocks, prolong)


def galerkin_buckets(a_blocks, ks, table, cols, prolong, bucket, bucket_count):
    slab_rows, unused_k, block_size, unused_size = a_blocks.shape
    n_k = len(ks)
    squeezed = pl.Squeezed()
    a_specs = [
        pl.BlockSpec((ROWS_PER_STEP, squeezed, block_size, block_size),
                     functools.partial(lambda k, s, b, c: (s, k, 0, 0), k))
        for k in ks
    ]
    right_specs = [
        pl.BlockSpec((squeezed, block_size, block_size),
                     functools.partial(lambda i, j, s, b, c: (c[s * ROWS_PER_STEP + i, j], 0, 0), i, j))
        for i in range(ROWS_PER_STEP)
        for j in range(n_k)
    ]
    pt_spec = pl.BlockSpec((ROWS_PER_STEP, block_size, block_size), lambda s, b, c: (s, 0, 0))
    out_spec = pl.BlockSpec(
        (bucket_count, n_k, block_size, block_size), lambda s, b, c: (0, 0, 0, 0)
    )
    flops = 4 * slab_rows * n_k * block_size ** 3
    moved = 2 * block_size * block_size * (slab_rows * (2 * n_k + 1) + bucket_count * n_k)
    return pl.pallas_call(
        functools.partial(galerkin_kernel, n_k),
        out_shape=jax.ShapeDtypeStruct((bucket_count, n_k, block_size, block_size), jnp.bfloat16),
        grid_spec=pltpu.PrefetchScalarGridSpec(
            num_scalar_prefetch=2,
            grid=(slab_rows // ROWS_PER_STEP,),
            in_specs=a_specs + right_specs + [pt_spec],
            out_specs=out_spec,
        ),
        compiler_params=pltpu.CompilerParams(dimension_semantics=("arbitrary",)),
        cost_estimate=pl.CostEstimate(flops=flops, bytes_accessed=moved, transcendentals=0),
    )(bucket, cols, *([a_blocks] * n_k), *([table] * (ROWS_PER_STEP * n_k)), prolong)


ACCUMULATORS = 4


def reduce_kernel(has_init, slot_ref, *refs):
    if has_init:
        init_ref, blocks_ref, out_ref = refs[:3]
    else:
        blocks_ref, out_ref = refs[:2]
    acc_refs = refs[-ACCUMULATORS:]
    slot_count = out_ref.shape[0]
    for acc_ref in acc_refs:
        acc_ref[...] = jnp.zeros_like(acc_ref)

    def add_blocks(index, carry):
        for j, acc_ref in enumerate(acc_refs):
            block = index * ACCUMULATORS + j
            slot = slot_ref[block]
            valid = (slot >= 0) & (slot < slot_count)
            target = jnp.clip(slot, 0, slot_count - 1)
            addend = jnp.where(valid, blocks_ref[block].astype(jnp.float32), 0.0)
            acc_ref[target] = acc_ref[target] + addend
        return carry

    lax.fori_loop(0, blocks_ref.shape[0] // ACCUMULATORS, add_blocks, 0, unroll=4)
    total = acc_refs[0][...]
    for acc_ref in acc_refs[1:]:
        total = total + acc_ref[...]
    if has_init:
        total = total + init_ref[...]
    out_ref[...] = total


def reduce_by_slot(slot_of_block, blocks, init=None):
    block_count, block_size, unused_size = blocks.shape
    whole = lambda shape: pl.BlockSpec(shape, lambda i, s: (0,) * len(shape))
    out_shape = (CB_DEV, block_size, block_size)
    in_specs = [whole(blocks.shape)]
    operands = [blocks]
    if init is not None:
        in_specs = [whole(out_shape)] + in_specs
        operands = [init] + operands
    return pl.pallas_call(
        functools.partial(reduce_kernel, init is not None),
        out_shape=jax.ShapeDtypeStruct(out_shape, jnp.float32),
        grid_spec=pltpu.PrefetchScalarGridSpec(
            num_scalar_prefetch=1,
            grid=(1,),
            in_specs=in_specs,
            out_specs=whole(out_shape),
            scratch_shapes=[pltpu.VMEM(out_shape, jnp.float32)] * ACCUMULATORS,
        ),
        cost_estimate=pl.CostEstimate(
            flops=block_count * block_size * block_size,
            bytes_accessed=blocks.size * 2 + 8 * CB_DEV * block_size * block_size,
            transcendentals=0,
        ),
    )(slot_of_block.astype(jnp.int32), *operands)


def per_device(a_blocks, a_cols, prolong, owners, slots):
    slab_rows, per_row, block_size, unused_size = a_blocks.shape
    owner_count = lax.axis_size("wide")
    bucket_count = owner_count * CAP_OWNER

    row_ids = jnp.arange(slab_rows, dtype=jnp.int32)
    same_owner = (owners[:, None] == owners[None, :]) & (row_ids[None, :] < row_ids[:, None])
    owner_position = jnp.sum(same_owner.astype(jnp.int32), axis=1)
    bucket = jnp.clip(owners * CAP_OWNER + owner_position, 0, bucket_count - 1).astype(jnp.int32)
    outgoing_diag = diag_buckets(a_blocks, prolong, slots, bucket, owner_count)
    arrived_diag = lax.all_to_all(outgoing_diag, "wide", split_axis=0, concat_axis=0, tiled=True)
    arrived_meta = arrived_diag[:, CAP_OWNER * block_size, : CAP_OWNER * per_row].astype(jnp.float32)
    arrived_slots = (jnp.round(arrived_meta).astype(jnp.int32) - 1).reshape(
        owner_count, CAP_OWNER, per_row
    )

    shard_blocks = lax.all_gather(prolong, "narrow", axis=0, tiled=True)
    piece_rows = shard_blocks.shape[0]
    off_cols = jnp.clip(a_cols[:, 1:], 0, piece_rows - 1).astype(jnp.int32)
    outgoing_off = galerkin_buckets(
        a_blocks, tuple(range(1, per_row)), shard_blocks, off_cols, prolong, bucket, bucket_count
    ).reshape(owner_count, CAP_OWNER * (per_row - 1), block_size, block_size)
    arrived_off = lax.all_to_all(outgoing_off, "wide", split_axis=0, concat_axis=0, tiled=True)

    coarse_diag = reduce_by_slot(
        arrived_slots[:, :, 0].reshape(-1),
        arrived_diag[:, : CAP_OWNER * block_size].reshape(-1, block_size, block_size),
    )
    coarse_sum = reduce_by_slot(
        arrived_slots[:, :, 1:].reshape(-1),
        arrived_off.reshape(-1, block_size, block_size),
        coarse_diag,
    )
    return coarse_sum.reshape(CB_DEV, block_size, block_size)


def solution(mesh):
    return jax.shard_map(
        per_device,
        mesh=mesh,
        in_specs=(
            P(("wide", "narrow"), None, None, None),
            P(("wide", "narrow"), None),
            P(("wide", "narrow"), None, None),
            P(("wide", "narrow")),
            P(("wide", "narrow"), None),
        ),
        out_specs=P(("wide", "narrow"), None, None),
        check_vma=False,
    )
```

```python
import functools

import jax
import jax.numpy as jnp
from jax import lax
from jax.experimental import pallas as pl
from jax.experimental.pallas import tpu as pltpu
from jax.sharding import PartitionSpec as P

CAP_OWNER = 2
CB_DEV = 24


ROWS_PER_STEP = 16


def galerkin_kernel(n_k, bucket_ref, cols_ref, *refs):
    a_refs = refs[:n_k]
    right_refs = refs[n_k:n_k + ROWS_PER_STEP * n_k]
    pt_ref = refs[n_k + ROWS_PER_STEP * n_k]
    out_ref = refs[n_k + ROWS_PER_STEP * n_k + 1]
    step = pl.program_id(0)

    @pl.when(step == 0)
    def _():
        out_ref[...] = jnp.zeros_like(out_ref)

    for i in range(ROWS_PER_STEP):
        bucket = bucket_ref[step * ROWS_PER_STEP + i]
        for k in range(n_k):
            product = jnp.dot(
                a_refs[k][i], right_refs[i * n_k + k][...], preferred_element_type=jnp.float32
            ).astype(jnp.bfloat16)
            galerkin = lax.dot_general(
                pt_ref[i], product, (((0,), (0,)), ((), ())), preferred_element_type=jnp.float32
            )
            out_ref[bucket, k] = galerkin.astype(jnp.bfloat16)


META_ROWS = 16


def diag_kernel(bucket_ref, slot_ref, a_ref, p_ref, out_ref):
    step = pl.program_id(0)
    block_size = p_ref.shape[-1]
    per_row = slot_ref.shape[1]

    @pl.when(step == 0)
    def _():
        out_ref[...] = jnp.zeros_like(out_ref)

    rows = lax.broadcasted_iota(jnp.int32, (META_ROWS, block_size), 0)
    cols = lax.broadcasted_iota(jnp.int32, (META_ROWS, block_size), 1)
    for i in range(ROWS_PER_STEP):
        row = step * ROWS_PER_STEP + i
        bucket = bucket_ref[row]
        owner = bucket // CAP_OWNER
        pos = bucket - owner * CAP_OWNER
        product = jnp.dot(a_ref[i], p_ref[i], preferred_element_type=jnp.float32).astype(jnp.bfloat16)
        galerkin = lax.dot_general(
            p_ref[i], product, (((0,), (0,)), ((), ())), preferred_element_type=jnp.float32
        )
        out_ref[owner, pl.ds(pl.multiple_of(pos * block_size, block_size), block_size), :] = (
            galerkin.astype(jnp.bfloat16)
        )
        meta = jnp.zeros((META_ROWS, block_size), jnp.int32)
        for k in range(per_row):
            meta = jnp.where((rows == 0) & (cols == pos * per_row + k), slot_ref[row, k] + 1, meta)
        meta_rows = pl.ds(CAP_OWNER * block_size, META_ROWS)
        out_ref[owner, meta_rows, :] = (
            out_ref[owner, meta_rows, :].astype(jnp.float32) + meta.astype(jnp.float32)
        ).astype(jnp.bfloat16)


def diag_buckets(a_blocks, prolong, slots, bucket, owner_count):
    slab_rows, per_row, block_size, unused_size = a_blocks.shape
    squeezed = pl.Squeezed()
    chunk_rows = CAP_OWNER * block_size + META_ROWS
    return pl.pallas_call(
        diag_kernel,
        out_shape=jax.ShapeDtypeStruct((owner_count, chunk_rows, block_size), jnp.bfloat16),
        grid_spec=pltpu.PrefetchScalarGridSpec(
            num_scalar_prefetch=2,
            grid=(slab_rows // ROWS_PER_STEP,),
            in_specs=[
                pl.BlockSpec((ROWS_PER_STEP, squeezed, block_size, block_size), lambda s, b, c: (s, 0, 0, 0)),
                pl.BlockSpec((ROWS_PER_STEP, block_size, block_size), lambda s, b, c: (s, 0, 0)),
            ],
            out_specs=pl.BlockSpec((owner_count, chunk_rows, block_size), lambda s, b, c: (0, 0, 0)),
        ),
        compiler_params=pltpu.CompilerParams(dimension_semantics=("arbitrary",)),
        cost_estimate=pl.CostEstimate(
            flops=4 * slab_rows * block_size ** 3,
            bytes_accessed=2 * block_size * (2 * slab_rows * block_size + owner_count * chunk_rows),
            transcendentals=0,
        ),
    )(bucket, slots.astype(jnp.int32), a_blocks, prolong)


def galerkin_buckets(a_blocks, ks, table, cols, prolong, bucket, bucket_count):
    slab_rows, unused_k, block_size, unused_size = a_blocks.shape
    n_k = len(ks)
    squeezed = pl.Squeezed()
    a_specs = [
        pl.BlockSpec((ROWS_PER_STEP, squeezed, block_size, block_size),
                     functools.partial(lambda k, s, b, c: (s, k, 0, 0), k))
        for k in ks
    ]
    right_specs = [
        pl.BlockSpec((squeezed, block_size, block_size),
                     functools.partial(lambda i, j, s, b, c: (c[s * ROWS_PER_STEP + i, j], 0, 0), i, j))
        for i in range(ROWS_PER_STEP)
        for j in range(n_k)
    ]
    pt_spec = pl.BlockSpec((ROWS_PER_STEP, block_size, block_size), lambda s, b, c: (s, 0, 0))
    out_spec = pl.BlockSpec(
        (bucket_count, n_k, block_size, block_size), lambda s, b, c: (0, 0, 0, 0)
    )
    flops = 4 * slab_rows * n_k * block_size ** 3
    moved = 2 * block_size * block_size * (slab_rows * (2 * n_k + 1) + bucket_count * n_k)
    return pl.pallas_call(
        functools.partial(galerkin_kernel, n_k),
        out_shape=jax.ShapeDtypeStruct((bucket_count, n_k, block_size, block_size), jnp.bfloat16),
        grid_spec=pltpu.PrefetchScalarGridSpec(
            num_scalar_prefetch=2,
            grid=(slab_rows // ROWS_PER_STEP,),
            in_specs=a_specs + right_specs + [pt_spec],
            out_specs=out_spec,
        ),
        compiler_params=pltpu.CompilerParams(dimension_semantics=("arbitrary",)),
        cost_estimate=pl.CostEstimate(flops=flops, bytes_accessed=moved, transcendentals=0),
    )(bucket, cols, *([a_blocks] * n_k), *([table] * (ROWS_PER_STEP * n_k)), prolong)


ACCUMULATORS = 4


def reduce_kernel(has_init, slot_ref, *refs):
    if has_init:
        init_ref, blocks_ref, out_ref = refs[:3]
    else:
        blocks_ref, out_ref = refs[:2]
    acc_refs = refs[-ACCUMULATORS:]
    slot_count = out_ref.shape[0]
    for acc_ref in acc_refs:
        acc_ref[...] = jnp.zeros_like(acc_ref)

    def add_blocks(index, carry):
        for j, acc_ref in enumerate(acc_refs):
            block = index * ACCUMULATORS + j
            slot = slot_ref[block]
            valid = (slot >= 0) & (slot < slot_count)
            target = jnp.clip(slot, 0, slot_count - 1)
            addend = jnp.where(valid, blocks_ref[block].astype(jnp.float32), 0.0)
            acc_ref[target] = acc_ref[target] + addend
        return carry

    lax.fori_loop(0, blocks_ref.shape[0] // ACCUMULATORS, add_blocks, 0, unroll=4)
    total = acc_refs[0][...]
    for acc_ref in acc_refs[1:]:
        total = total + acc_ref[...]
    if has_init:
        total = total + init_ref[...]
    out_ref[...] = total


def reduce_by_slot(slot_of_block, blocks, init=None):
    block_count, block_size, unused_size = blocks.shape
    whole = lambda shape: pl.BlockSpec(shape, lambda i, s: (0,) * len(shape))
    out_shape = (CB_DEV, block_size, block_size)
    in_specs = [whole(blocks.shape)]
    operands = [blocks]
    if init is not None:
        in_specs = [whole(out_shape)] + in_specs
        operands = [init] + operands
    return pl.pallas_call(
        functools.partial(reduce_kernel, init is not None),
        out_shape=jax.ShapeDtypeStruct(out_shape, jnp.float32),
        grid_spec=pltpu.PrefetchScalarGridSpec(
            num_scalar_prefetch=1,
            grid=(1,),
            in_specs=in_specs,
            out_specs=whole(out_shape),
            scratch_shapes=[pltpu.VMEM(out_shape, jnp.float32)] * ACCUMULATORS,
        ),
        cost_estimate=pl.CostEstimate(
            flops=block_count * block_size * block_size,
            bytes_accessed=blocks.size * 2 + 8 * CB_DEV * block_size * block_size,
            transcendentals=0,
        ),
    )(slot_of_block.astype(jnp.int32), *operands)


def per_device(a_blocks, a_cols, prolong, owners, slots):
    slab_rows, per_row, block_size, unused_size = a_blocks.shape
    owner_count = lax.axis_size("wide")
    bucket_count = owner_count * CAP_OWNER

    row_ids = jnp.arange(slab_rows, dtype=jnp.int32)
    same_owner = (owners[:, None] == owners[None, :]) & (row_ids[None, :] < row_ids[:, None])
    owner_position = jnp.sum(same_owner.astype(jnp.int32), axis=1)
    bucket = jnp.clip(owners * CAP_OWNER + owner_position, 0, bucket_count - 1).astype(jnp.int32)
    outgoing_diag = diag_buckets(a_blocks, prolong, slots, bucket, owner_count)
    arrived_diag = lax.all_to_all(outgoing_diag, "wide", split_axis=0, concat_axis=0, tiled=True)
    arrived_meta = arrived_diag[:, CAP_OWNER * block_size, : CAP_OWNER * per_row].astype(jnp.float32)
    arrived_slots = (jnp.round(arrived_meta).astype(jnp.int32) - 1).reshape(
        owner_count, CAP_OWNER, per_row
    )

    shard_blocks = lax.all_gather(prolong, "narrow", axis=0, tiled=True)
    piece_rows = shard_blocks.shape[0]
    off_cols = jnp.clip(a_cols[:, 1:], 0, piece_rows - 1).astype(jnp.int32)
    outgoing_off = galerkin_buckets(
        a_blocks, tuple(range(1, per_row)), shard_blocks, off_cols, prolong, bucket, bucket_count
    ).reshape(owner_count, CAP_OWNER * (per_row - 1), block_size, block_size)
    arrived_off = lax.all_to_all(outgoing_off, "wide", split_axis=0, concat_axis=0, tiled=True)

    coarse_diag = reduce_by_slot(
        arrived_slots[:, :, 0].reshape(-1),
        arrived_diag[:, : CAP_OWNER * block_size].reshape(-1, block_size, block_size),
    )
    coarse_sum = reduce_by_slot(
        arrived_slots[:, :, 1:].reshape(-1),
        arrived_off.reshape(-1, block_size, block_size),
        coarse_diag,
    )
    return coarse_sum.reshape(CB_DEV, block_size, block_size)


def solution(mesh):
    return jax.shard_map(
        per_device,
        mesh=mesh,
        in_specs=(
            P(("wide", "narrow"), None, None, None),
            P(("wide", "narrow"), None),
            P(("wide", "narrow"), None, None),
            P(("wide", "narrow")),
            P(("wide", "narrow"), None),
        ),
        out_specs=P(("wide", "narrow"), None, None),
        check_vma=False,
    )
```

```python
import functools

import jax
import jax.numpy as jnp
from jax import lax
from jax.experimental import pallas as pl
from jax.experimental.pallas import tpu as pltpu
from jax.sharding import PartitionSpec as P

CAP_OWNER = 2
CB_DEV = 24


ROWS_PER_STEP = 16


def galerkin_kernel(n_k, bucket_ref, cols_ref, *refs):
    a_refs = refs[:n_k]
    right_refs = refs[n_k:n_k + ROWS_PER_STEP * n_k]
    pt_ref = refs[n_k + ROWS_PER_STEP * n_k]
    out_ref = refs[n_k + ROWS_PER_STEP * n_k + 1]
    step = pl.program_id(0)

    @pl.when(step == 0)
    def _():
        out_ref[...] = jnp.zeros_like(out_ref)

    for i in range(ROWS_PER_STEP):
        bucket = bucket_ref[step * ROWS_PER_STEP + i]
        for k in range(n_k):
            product = jnp.dot(
                a_refs[k][i], right_refs[i * n_k + k][...], preferred_element_type=jnp.float32
            ).astype(jnp.bfloat16)
            galerkin = lax.dot_general(
                pt_ref[i], product, (((0,), (0,)), ((), ())), preferred_element_type=jnp.float32
            )
            out_ref[bucket, k] = galerkin.astype(jnp.bfloat16)


META_ROWS = 16


def diag_kernel(owner_ref, slot_ref, a_ref, p_ref, out_ref):
    step = pl.program_id(0)
    block_size = p_ref.shape[-1]
    per_row = slot_ref.shape[1]

    @pl.when(step == 0)
    def _():
        out_ref[...] = jnp.zeros_like(out_ref)

    rows = lax.broadcasted_iota(jnp.int32, (META_ROWS, block_size), 0)
    cols = lax.broadcasted_iota(jnp.int32, (META_ROWS, block_size), 1)
    for i in range(ROWS_PER_STEP):
        row = step * ROWS_PER_STEP + i
        owner = owner_ref[row]
        pos = jnp.int32(0)
        for j in range(owner_ref.shape[0]):
            pos = pos + jnp.where((j < row) & (owner_ref[j] == owner), 1, 0).astype(jnp.int32)
        bucket = jnp.clip(owner * CAP_OWNER + pos, 0, out_ref.shape[0] * CAP_OWNER - 1)
        owner = bucket // CAP_OWNER
        pos = bucket - owner * CAP_OWNER
        product = jnp.dot(a_ref[i], p_ref[i], preferred_element_type=jnp.float32).astype(jnp.bfloat16)
        galerkin = lax.dot_general(
            p_ref[i], product, (((0,), (0,)), ((), ())), preferred_element_type=jnp.float32
        )
        out_ref[owner, pl.ds(pl.multiple_of(pos * block_size, block_size), block_size), :] = (
            galerkin.astype(jnp.bfloat16)
        )
        meta = jnp.zeros((META_ROWS, block_size), jnp.int32)
        for k in range(per_row):
            meta = jnp.where((rows == 0) & (cols == pos * per_row + k), slot_ref[row, k] + 1, meta)
        meta_rows = pl.ds(CAP_OWNER * block_size, META_ROWS)
        out_ref[owner, meta_rows, :] = (
            out_ref[owner, meta_rows, :].astype(jnp.float32) + meta.astype(jnp.float32)
        ).astype(jnp.bfloat16)


def diag_buckets(a_blocks, prolong, slots, owners, owner_count):
    slab_rows, per_row, block_size, unused_size = a_blocks.shape
    squeezed = pl.Squeezed()
    chunk_rows = CAP_OWNER * block_size + META_ROWS
    return pl.pallas_call(
        diag_kernel,
        out_shape=jax.ShapeDtypeStruct((owner_count, chunk_rows, block_size), jnp.bfloat16),
        grid_spec=pltpu.PrefetchScalarGridSpec(
            num_scalar_prefetch=2,
            grid=(slab_rows // ROWS_PER_STEP,),
            in_specs=[
                pl.BlockSpec((ROWS_PER_STEP, squeezed, block_size, block_size), lambda s, b, c: (s, 0, 0, 0)),
                pl.BlockSpec((ROWS_PER_STEP, block_size, block_size), lambda s, b, c: (s, 0, 0)),
            ],
            out_specs=pl.BlockSpec((owner_count, chunk_rows, block_size), lambda s, b, c: (0, 0, 0)),
        ),
        compiler_params=pltpu.CompilerParams(dimension_semantics=("arbitrary",)),
        cost_estimate=pl.CostEstimate(
            flops=4 * slab_rows * block_size ** 3,
            bytes_accessed=2 * block_size * (2 * slab_rows * block_size + owner_count * chunk_rows),
            transcendentals=0,
        ),
    )(owners.astype(jnp.int32), slots.astype(jnp.int32), a_blocks, prolong)


def galerkin_buckets(a_blocks, ks, table, cols, prolong, bucket, bucket_count):
    slab_rows, unused_k, block_size, unused_size = a_blocks.shape
    n_k = len(ks)
    squeezed = pl.Squeezed()
    a_specs = [
        pl.BlockSpec((ROWS_PER_STEP, squeezed, block_size, block_size),
                     functools.partial(lambda k, s, b, c: (s, k, 0, 0), k))
        for k in ks
    ]
    right_specs = [
        pl.BlockSpec((squeezed, block_size, block_size),
                     functools.partial(lambda i, j, s, b, c: (c[s * ROWS_PER_STEP + i, j], 0, 0), i, j))
        for i in range(ROWS_PER_STEP)
        for j in range(n_k)
    ]
    pt_spec = pl.BlockSpec((ROWS_PER_STEP, block_size, block_size), lambda s, b, c: (s, 0, 0))
    out_spec = pl.BlockSpec(
        (bucket_count, n_k, block_size, block_size), lambda s, b, c: (0, 0, 0, 0)
    )
    flops = 4 * slab_rows * n_k * block_size ** 3
    moved = 2 * block_size * block_size * (slab_rows * (2 * n_k + 1) + bucket_count * n_k)
    return pl.pallas_call(
        functools.partial(galerkin_kernel, n_k),
        out_shape=jax.ShapeDtypeStruct((bucket_count, n_k, block_size, block_size), jnp.bfloat16),
        grid_spec=pltpu.PrefetchScalarGridSpec(
            num_scalar_prefetch=2,
            grid=(slab_rows // ROWS_PER_STEP,),
            in_specs=a_specs + right_specs + [pt_spec],
            out_specs=out_spec,
        ),
        compiler_params=pltpu.CompilerParams(dimension_semantics=("arbitrary",)),
        cost_estimate=pl.CostEstimate(flops=flops, bytes_accessed=moved, transcendentals=0),
    )(bucket, cols, *([a_blocks] * n_k), *([table] * (ROWS_PER_STEP * n_k)), prolong)


ACCUMULATORS = 4


def reduce_kernel(has_init, slot_ref, *refs):
    if has_init:
        init_ref, blocks_ref, out_ref = refs[:3]
    else:
        blocks_ref, out_ref = refs[:2]
    acc_refs = refs[-ACCUMULATORS:]
    slot_count = out_ref.shape[0]
    for acc_ref in acc_refs:
        acc_ref[...] = jnp.zeros_like(acc_ref)

    def add_blocks(index, carry):
        for j, acc_ref in enumerate(acc_refs):
            block = index * ACCUMULATORS + j
            slot = slot_ref[block]
            valid = (slot >= 0) & (slot < slot_count)
            target = jnp.clip(slot, 0, slot_count - 1)
            addend = jnp.where(valid, blocks_ref[block].astype(jnp.float32), 0.0)
            acc_ref[target] = acc_ref[target] + addend
        return carry

    lax.fori_loop(0, blocks_ref.shape[0] // ACCUMULATORS, add_blocks, 0, unroll=4)
    total = acc_refs[0][...]
    for acc_ref in acc_refs[1:]:
        total = total + acc_ref[...]
    if has_init:
        total = total + init_ref[...]
    out_ref[...] = total


def reduce_by_slot(slot_of_block, blocks, init=None):
    block_count, block_size, unused_size = blocks.shape
    whole = lambda shape: pl.BlockSpec(shape, lambda i, s: (0,) * len(shape))
    out_shape = (CB_DEV, block_size, block_size)
    in_specs = [whole(blocks.shape)]
    operands = [blocks]
    if init is not None:
        in_specs = [whole(out_shape)] + in_specs
        operands = [init] + operands
    return pl.pallas_call(
        functools.partial(reduce_kernel, init is not None),
        out_shape=jax.ShapeDtypeStruct(out_shape, jnp.float32),
        grid_spec=pltpu.PrefetchScalarGridSpec(
            num_scalar_prefetch=1,
            grid=(1,),
            in_specs=in_specs,
            out_specs=whole(out_shape),
            scratch_shapes=[pltpu.VMEM(out_shape, jnp.float32)] * ACCUMULATORS,
        ),
        cost_estimate=pl.CostEstimate(
            flops=block_count * block_size * block_size,
            bytes_accessed=blocks.size * 2 + 8 * CB_DEV * block_size * block_size,
            transcendentals=0,
        ),
    )(slot_of_block.astype(jnp.int32), *operands)


def per_device(a_blocks, a_cols, prolong, owners, slots):
    slab_rows, per_row, block_size, unused_size = a_blocks.shape
    owner_count = lax.axis_size("wide")
    bucket_count = owner_count * CAP_OWNER

    row_ids = jnp.arange(slab_rows, dtype=jnp.int32)
    same_owner = (owners[:, None] == owners[None, :]) & (row_ids[None, :] < row_ids[:, None])
    owner_position = jnp.sum(same_owner.astype(jnp.int32), axis=1)
    bucket = jnp.clip(owners * CAP_OWNER + owner_position, 0, bucket_count - 1).astype(jnp.int32)
    outgoing_diag = diag_buckets(a_blocks, prolong, slots, owners, owner_count)
    arrived_diag = lax.all_to_all(outgoing_diag, "wide", split_axis=0, concat_axis=0, tiled=True)
    arrived_meta = arrived_diag[:, CAP_OWNER * block_size, : CAP_OWNER * per_row].astype(jnp.float32)
    arrived_slots = (jnp.round(arrived_meta).astype(jnp.int32) - 1).reshape(
        owner_count, CAP_OWNER, per_row
    )

    shard_blocks = lax.all_gather(prolong, "narrow", axis=0, tiled=True)
    piece_rows = shard_blocks.shape[0]
    off_cols = jnp.clip(a_cols[:, 1:], 0, piece_rows - 1).astype(jnp.int32)
    outgoing_off = galerkin_buckets(
        a_blocks, tuple(range(1, per_row)), shard_blocks, off_cols, prolong, bucket, bucket_count
    ).reshape(owner_count, CAP_OWNER * (per_row - 1), block_size, block_size)
    arrived_off = lax.all_to_all(outgoing_off, "wide", split_axis=0, concat_axis=0, tiled=True)

    coarse_diag = reduce_by_slot(
        arrived_slots[:, :, 0].reshape(-1),
        arrived_diag[:, : CAP_OWNER * block_size].reshape(-1, block_size, block_size),
    )
    coarse_sum = reduce_by_slot(
        arrived_slots[:, :, 1:].reshape(-1),
        arrived_off.reshape(-1, block_size, block_size),
        coarse_diag,
    )
    return coarse_sum.reshape(CB_DEV, block_size, block_size)


def solution(mesh):
    return jax.shard_map(
        per_device,
        mesh=mesh,
        in_specs=(
            P(("wide", "narrow"), None, None, None),
            P(("wide", "narrow"), None),
            P(("wide", "narrow"), None, None),
            P(("wide", "narrow")),
            P(("wide", "narrow"), None),
        ),
        out_specs=P(("wide", "narrow"), None, None),
        check_vma=False,
    )
```

```python
import functools

import jax
import jax.numpy as jnp
from jax import lax
from jax.experimental import pallas as pl
from jax.experimental.pallas import tpu as pltpu
from jax.sharding import PartitionSpec as P

CAP_OWNER = 2
CB_DEV = 24


ROWS_PER_STEP = 16


def galerkin_kernel(n_k, bucket_ref, cols_ref, *refs):
    a_refs = refs[:n_k]
    right_refs = refs[n_k:n_k + ROWS_PER_STEP * n_k]
    pt_ref = refs[n_k + ROWS_PER_STEP * n_k]
    out_ref, stage_ref, sems = refs[n_k + ROWS_PER_STEP * n_k + 2:]
    step = pl.program_id(0)
    copies = []
    for i in range(ROWS_PER_STEP):
        bucket = bucket_ref[step * ROWS_PER_STEP + i]
        for k in range(n_k):
            product = jnp.dot(
                a_refs[k][i], right_refs[i * n_k + k][...], preferred_element_type=jnp.float32
            ).astype(jnp.bfloat16)
            galerkin = lax.dot_general(
                pt_ref[i], product, (((0,), (0,)), ((), ())), preferred_element_type=jnp.float32
            )
            slot = i * n_k + k
            stage_ref[slot] = galerkin.astype(jnp.bfloat16)
            copy = pltpu.make_async_copy(stage_ref.at[slot], out_ref.at[bucket, k], sems.at[slot])
            copy.start()
            copies.append(copy)
    for copy in copies:
        copy.wait()


META_ROWS = 16


def diag_kernel(owner_ref, slot_ref, a_ref, p_ref, out_ref):
    step = pl.program_id(0)
    block_size = p_ref.shape[-1]
    per_row = slot_ref.shape[1]

    @pl.when(step == 0)
    def _():
        out_ref[...] = jnp.zeros_like(out_ref)

    rows = lax.broadcasted_iota(jnp.int32, (META_ROWS, block_size), 0)
    cols = lax.broadcasted_iota(jnp.int32, (META_ROWS, block_size), 1)
    for i in range(ROWS_PER_STEP):
        row = step * ROWS_PER_STEP + i
        owner = owner_ref[row]
        pos = jnp.int32(0)
        for j in range(owner_ref.shape[0]):
            pos = pos + jnp.where((j < row) & (owner_ref[j] == owner), 1, 0).astype(jnp.int32)
        bucket = jnp.clip(owner * CAP_OWNER + pos, 0, out_ref.shape[0] * CAP_OWNER - 1)
        owner = bucket // CAP_OWNER
        pos = bucket - owner * CAP_OWNER
        product = jnp.dot(a_ref[i], p_ref[i], preferred_element_type=jnp.float32).astype(jnp.bfloat16)
        galerkin = lax.dot_general(
            p_ref[i], product, (((0,), (0,)), ((), ())), preferred_element_type=jnp.float32
        )
        out_ref[owner, pl.ds(pl.multiple_of(pos * block_size, block_size), block_size), :] = (
            galerkin.astype(jnp.bfloat16)
        )
        meta = jnp.zeros((META_ROWS, block_size), jnp.int32)
        for k in range(per_row):
            meta = jnp.where((rows == 0) & (cols == pos * per_row + k), slot_ref[row, k] + 1, meta)
        meta_rows = pl.ds(CAP_OWNER * block_size, META_ROWS)
        out_ref[owner, meta_rows, :] = (
            out_ref[owner, meta_rows, :].astype(jnp.float32) + meta.astype(jnp.float32)
        ).astype(jnp.bfloat16)


def diag_buckets(a_blocks, prolong, slots, owners, owner_count):
    slab_rows, per_row, block_size, unused_size = a_blocks.shape
    squeezed = pl.Squeezed()
    chunk_rows = CAP_OWNER * block_size + META_ROWS
    return pl.pallas_call(
        diag_kernel,
        out_shape=jax.ShapeDtypeStruct((owner_count, chunk_rows, block_size), jnp.bfloat16),
        grid_spec=pltpu.PrefetchScalarGridSpec(
            num_scalar_prefetch=2,
            grid=(slab_rows // ROWS_PER_STEP,),
            in_specs=[
                pl.BlockSpec((ROWS_PER_STEP, squeezed, block_size, block_size), lambda s, b, c: (s, 0, 0, 0)),
                pl.BlockSpec((ROWS_PER_STEP, block_size, block_size), lambda s, b, c: (s, 0, 0)),
            ],
            out_specs=pl.BlockSpec((owner_count, chunk_rows, block_size), lambda s, b, c: (0, 0, 0)),
        ),
        compiler_params=pltpu.CompilerParams(dimension_semantics=("arbitrary",)),
        cost_estimate=pl.CostEstimate(
            flops=4 * slab_rows * block_size ** 3,
            bytes_accessed=2 * block_size * (2 * slab_rows * block_size + owner_count * chunk_rows),
            transcendentals=0,
        ),
    )(owners.astype(jnp.int32), slots.astype(jnp.int32), a_blocks, prolong)


def galerkin_buckets(a_blocks, ks, table, cols, prolong, bucket, bucket_count):
    slab_rows, unused_k, block_size, unused_size = a_blocks.shape
    n_k = len(ks)
    squeezed = pl.Squeezed()
    a_specs = [
        pl.BlockSpec((ROWS_PER_STEP, squeezed, block_size, block_size),
                     functools.partial(lambda k, s, b, c: (s, k, 0, 0), k))
        for k in ks
    ]
    right_specs = [
        pl.BlockSpec((squeezed, block_size, block_size),
                     functools.partial(lambda i, j, s, b, c: (c[s * ROWS_PER_STEP + i, j], 0, 0), i, j))
        for i in range(ROWS_PER_STEP)
        for j in range(n_k)
    ]
    pt_spec = pl.BlockSpec((ROWS_PER_STEP, block_size, block_size), lambda s, b, c: (s, 0, 0))
    any_spec = pl.BlockSpec(memory_space=pl.ANY)
    flops = 4 * slab_rows * n_k * block_size ** 3
    moved = 2 * block_size * block_size * slab_rows * (3 * n_k + 1)
    zeros = jnp.zeros((bucket_count, n_k, block_size, block_size), jnp.bfloat16)
    return pl.pallas_call(
        functools.partial(galerkin_kernel, n_k),
        out_shape=jax.ShapeDtypeStruct((bucket_count, n_k, block_size, block_size), jnp.bfloat16),
        grid_spec=pltpu.PrefetchScalarGridSpec(
            num_scalar_prefetch=2,
            grid=(slab_rows // ROWS_PER_STEP,),
            in_specs=a_specs + right_specs + [pt_spec, any_spec],
            out_specs=any_spec,
            scratch_shapes=[
                pltpu.VMEM((ROWS_PER_STEP * n_k, block_size, block_size), jnp.bfloat16),
                pltpu.SemaphoreType.DMA((ROWS_PER_STEP * n_k,)),
            ],
        ),
        input_output_aliases={2 + n_k + ROWS_PER_STEP * n_k + 1: 0},
        compiler_params=pltpu.CompilerParams(dimension_semantics=("arbitrary",)),
        cost_estimate=pl.CostEstimate(flops=flops, bytes_accessed=moved, transcendentals=0),
    )(bucket, cols, *([a_blocks] * n_k), *([table] * (ROWS_PER_STEP * n_k)), prolong, zeros)


ACCUMULATORS = 4


def reduce_kernel(has_init, slot_ref, *refs):
    if has_init:
        init_ref, blocks_ref, out_ref = refs[:3]
    else:
        blocks_ref, out_ref = refs[:2]
    acc_refs = refs[-ACCUMULATORS:]
    slot_count = out_ref.shape[0]
    for acc_ref in acc_refs:
        acc_ref[...] = jnp.zeros_like(acc_ref)

    def add_blocks(index, carry):
        for j, acc_ref in enumerate(acc_refs):
            block = index * ACCUMULATORS + j
            slot = slot_ref[block]
            valid = (slot >= 0) & (slot < slot_count)
            target = jnp.clip(slot, 0, slot_count - 1)
            addend = jnp.where(valid, blocks_ref[block].astype(jnp.float32), 0.0)
            acc_ref[target] = acc_ref[target] + addend
        return carry

    lax.fori_loop(0, blocks_ref.shape[0] // ACCUMULATORS, add_blocks, 0, unroll=4)
    total = acc_refs[0][...]
    for acc_ref in acc_refs[1:]:
        total = total + acc_ref[...]
    if has_init:
        total = total + init_ref[...]
    out_ref[...] = total


def reduce_by_slot(slot_of_block, blocks, init=None):
    block_count, block_size, unused_size = blocks.shape
    whole = lambda shape: pl.BlockSpec(shape, lambda i, s: (0,) * len(shape))
    out_shape = (CB_DEV, block_size, block_size)
    in_specs = [whole(blocks.shape)]
    operands = [blocks]
    if init is not None:
        in_specs = [whole(out_shape)] + in_specs
        operands = [init] + operands
    return pl.pallas_call(
        functools.partial(reduce_kernel, init is not None),
        out_shape=jax.ShapeDtypeStruct(out_shape, jnp.float32),
        grid_spec=pltpu.PrefetchScalarGridSpec(
            num_scalar_prefetch=1,
            grid=(1,),
            in_specs=in_specs,
            out_specs=whole(out_shape),
            scratch_shapes=[pltpu.VMEM(out_shape, jnp.float32)] * ACCUMULATORS,
        ),
        cost_estimate=pl.CostEstimate(
            flops=block_count * block_size * block_size,
            bytes_accessed=blocks.size * 2 + 8 * CB_DEV * block_size * block_size,
            transcendentals=0,
        ),
    )(slot_of_block.astype(jnp.int32), *operands)


def per_device(a_blocks, a_cols, prolong, owners, slots):
    slab_rows, per_row, block_size, unused_size = a_blocks.shape
    owner_count = lax.axis_size("wide")
    bucket_count = owner_count * CAP_OWNER

    row_ids = jnp.arange(slab_rows, dtype=jnp.int32)
    same_owner = (owners[:, None] == owners[None, :]) & (row_ids[None, :] < row_ids[:, None])
    owner_position = jnp.sum(same_owner.astype(jnp.int32), axis=1)
    bucket = jnp.clip(owners * CAP_OWNER + owner_position, 0, bucket_count - 1).astype(jnp.int32)
    outgoing_diag = diag_buckets(a_blocks, prolong, slots, owners, owner_count)
    arrived_diag = lax.all_to_all(outgoing_diag, "wide", split_axis=0, concat_axis=0, tiled=True)
    arrived_meta = arrived_diag[:, CAP_OWNER * block_size, : CAP_OWNER * per_row].astype(jnp.float32)
    arrived_slots = (jnp.round(arrived_meta).astype(jnp.int32) - 1).reshape(
        owner_count, CAP_OWNER, per_row
    )

    shard_blocks = lax.all_gather(prolong, "narrow", axis=0, tiled=True)
    piece_rows = shard_blocks.shape[0]
    off_cols = jnp.clip(a_cols[:, 1:], 0, piece_rows - 1).astype(jnp.int32)
    outgoing_off = galerkin_buckets(
        a_blocks, tuple(range(1, per_row)), shard_blocks, off_cols, prolong, bucket, bucket_count
    ).reshape(owner_count, CAP_OWNER * (per_row - 1), block_size, block_size)
    arrived_off = lax.all_to_all(outgoing_off, "wide", split_axis=0, concat_axis=0, tiled=True)

    coarse_diag = reduce_by_slot(
        arrived_slots[:, :, 0].reshape(-1),
        arrived_diag[:, : CAP_OWNER * block_size].reshape(-1, block_size, block_size),
    )
    coarse_sum = reduce_by_slot(
        arrived_slots[:, :, 1:].reshape(-1),
        arrived_off.reshape(-1, block_size, block_size),
        coarse_diag,
    )
    return coarse_sum.reshape(CB_DEV, block_size, block_size)


def solution(mesh):
    return jax.shard_map(
        per_device,
        mesh=mesh,
        in_specs=(
            P(("wide", "narrow"), None, None, None),
            P(("wide", "narrow"), None),
            P(("wide", "narrow"), None, None),
            P(("wide", "narrow")),
            P(("wide", "narrow"), None),
        ),
        out_specs=P(("wide", "narrow"), None, None),
        check_vma=False,
    )
```
